32 devices in a mesh: stream: 4 (over y, core), cross: 2 (over x), gore: 4 (over z).
Axes of the slice: x: 2, y: 2, z: 4, core: 2. Of those that a mesh axis runs over, the one named last changes fastest.
Arguments:
- density: float32 [16, 8, 512], P('stream', 'cross', 'gore'), may hold values from 1 to 2
- momentum_energy: float32 [4, 16, 8, 512], P(None, 'stream', 'cross', 'gore'), may hold values from -6 to 6
- viscosity: float32 [16, 8, 512], P('stream', 'cross', 'gore'), may hold values from 0.02 to 0.15
- records: float32 [8, 2048, 128], P(None, ('stream', 'cross', 'gore')), may hold values from -6 to 6
- cell_ids: int32 [2048, 128], P(('stream', 'cross', 'gore')), may hold values from 0 to 2047
- routes: int32 [2048, 1], P(('stream', 'cross', 'gore')), may hold values from 0 to 7; in each aligned block of 64 rows (0 to 63, 64 to 127, ...) at most 16 rows name the same one
- lengths: int32 [2048], P(('stream', 'cross', 'gore')), may hold values from 1 to 128, 163840 in all
Outputs:
- new_state: float32 [5, 16, 8, 512], P(None, 'stream', 'cross', 'gore')
- face_loads: float32 [3, 2048, 128], P(None, ('stream', 'cross', 'gore'))
The draws below stay inside these ranges and needn't reach their ends.
Inputs may be any that keep to these rules, and one draw needn't show every extreme that they name: `routes`: among the 64 tiles of one device no fluid block is named more than 16 times, and some block exactly 16 times. `lengths`: some tile is full.
All inputs are finite; a program needn't handle non-finite values. No bound on the sum of `lengths` on one device may be relied on, other than what follows from the above.
Results may differ from the reference program's by a relative error of at most 0.0003.
Values sent between devices are 32-bit elements; how exact they have to be, the bound alone decides.
No kernel may reach another device: no remote copies, remote signals or barrier semaphores. Data moves between devices by JAX's collectives and lax.ppermute only.
A program may use at most 64 MiB of HBM per device.

```python
import math
import jax
import jax.numpy as jnp
import numpy as np
from jax import lax

CX = 4
CY = 4
CZ = 128
TILES_DEV = 64
TILE_ROWS = 128
FIELDS = 8
BLOCKS = 8
CAP = 16
NX = 16
NY = 8
NZ = 512
TILES = 2048
N_CROSS = 2
N_GORE = 4


def with_ends(drawn, own_key, least, top_value):
    longest = drawn.shape.index(max(drawn.shape))
    spots = []
    for shift in (0, 1):
        where = [jax.random.randint(jax.random.fold_in(own_key, axis), (), 0, length) for axis, length in enumerate(drawn.shape)]
        where[longest] = (where[longest] + shift) % drawn.shape[longest]
        spots.append(tuple(where))
    return drawn.at[spots[0]].set(least).at[spots[1]].set(top_value)


def steps_of(own_key, shape, split, low, top_value):
    gain, own = 1.0, jax.random.fold_in(own_key, 6)
    for dim, blocks in split:
        steps = jnp.exp(jax.random.uniform(jax.random.fold_in(own, dim), (blocks,), jnp.float32, low / len(split), top_value / len(split)))
        gain = gain * jnp.repeat(steps, shape[dim] // blocks).reshape([-1 if axis == dim else 1 for axis in range(len(shape))])
    return gain


def profile(count, total, bound, skew):
    portions = [(1 << 20) // math.isqrt(grade ** skew) + 1 for grade in range(2, count + 1)]
    surplus, holding = total - bound - (count - 1), [1] * (count - 1)
    while surplus > 0:
        movable = [i for i in range(count - 1) if holding[i] < bound]
        mass, budget = sum([portions[i] for i in movable]), surplus
        for i in movable:
            extra = min(bound - holding[i], max(1, budget * portions[i] // mass), surplus)
            holding[i] = holding[i] + extra
            surplus = surplus - extra
    return np.array([bound] + holding)


def ragged(stream_key, count, total, most, skew):
    if count == 2:
        one = jax.random.randint(stream_key, (), max(1, total - most), min(most, total - 1) + 1)
        return jnp.stack([one, total - one])
    sizes = jnp.asarray(profile(count, total, most, skew), jnp.int32)
    couples = (count - 1) // 2
    giver, receiver = sizes[1:1 + 2 * couples:2], sizes[2:2 + 2 * couples:2]
    margin = jnp.minimum(giver - 1, most - receiver)
    moved = jax.random.randint(jax.random.fold_in(stream_key, 1), (couples,), 0, 1 << 20) % (margin + 1)
    sizes = sizes.at[1:1 + 2 * couples:2].set(giver - moved).at[2:2 + 2 * couples:2].set(receiver + moved)
    return sizes[jax.random.permutation(jax.random.fold_in(stream_key, 2), count)]


def shared_out(rng, own, number, rows, number_of, top, limit, lean):
    sequence = jax.random.permutation(rng, number_of)
    packed, ordinary = load_shares(number_of, rows * top, limit, lean, True), load_shares(number_of, rows * top, limit, lean, False)
    places = jnp.arange(number_of)

    def named(sizes, rotation):
        used = int((sizes > 0).sum())
        fixed = max(1, used // 4)
        moved = fixed + (places - fixed + rotation * (used - fixed)) % max(1, number_of - fixed)
        return jnp.zeros((number_of,), jnp.int32).at[sequence[jnp.where(places < fixed, places, moved)]].set(jnp.asarray(sizes, jnp.int32))

    sizes = jnp.where(number % 4 == 0, named(packed, number // 4), named(ordinary, number - number // 4 - 1))
    mixed = jax.random.permutation(jax.random.fold_in(own, 3), number_of)
    giver, receiver = mixed[0:number_of // 2 * 2:2], mixed[1:number_of // 2 * 2:2]
    room = jnp.minimum(sizes[giver] - 1, limit - sizes[receiver]) // 2
    room = jnp.where((giver == sequence[0]) | (receiver == sequence[0]) | (sizes[receiver] == 0), 0, jnp.maximum(room, 0))
    moved = jax.random.randint(jax.random.fold_in(own, 4), (number_of // 2,), 0, 1 << 20) % (room + 1)
    sizes = sizes.at[giver].add(-moved).at[receiver].add(moved)
    labels = jnp.searchsorted(jnp.cumsum(sizes), jnp.arange(rows * top), side="right").astype(jnp.int32)
    grid = labels.reshape(top, rows).T
    grid = grid[jax.random.permutation(jax.random.fold_in(own, 1), rows)]
    rotation = jax.random.randint(jax.random.fold_in(own, 2), (rows, 1), 0, top)
    return jnp.take_along_axis(grid, (jnp.arange(top)[None, :] + rotation) % top, axis=1)


def load_shares(amount, total, limit, skew, full):
    portions = [(1 << 20) // math.isqrt(rank ** skew) + 1 for rank in range(1, amount + 1)]
    largest = limit if full else min(limit, max(-(-total // amount), total * portions[0] // sum(portions)))
    least = 1 if total - largest >= amount - 1 else 0
    given, surplus = [largest] + [least] * (amount - 1), total - largest - least * (amount - 1)
    while surplus > 0:
        free = [i for i in range(1, amount) if given[i] < largest] or [i for i in range(1, amount) if given[i] < limit]
        pool, remaining = sum([portions[i] for i in free]), surplus
        for i in free:
            extra = min(limit - given[i], max(1, remaining * portions[i] // pool), surplus)
            given[i] = given[i] + extra
            surplus = surplus - extra
    return np.array(given)


def bell_draw(key, shape, scale, bound, cuts=(), kind=jnp.bfloat16):
    loudness = steps_of(key, shape, cuts, -0.22, 0.18) if cuts else 1.0
    entries = jax.random.normal(key, shape, jnp.float32) * scale * loudness
    return jnp.minimum(jnp.maximum(entries, -bound), bound).astype(kind)


def setup_inputs(seed: int = 0) -> dict:
    streams_of = jax.random.split(jax.random.key(seed), 8)
    density = jnp.clip(1.0 + 1.0 * jax.random.uniform(streams_of[0], (NX, NY, NZ), jnp.float32) ** steps_of(streams_of[0], (NX, NY, NZ), ((0, 4), (1, 2), (2, 4)), -0.2, 0.2), 1.0, 2.0)
    momentum_energy = bell_draw(streams_of[1], (4, NX, NY, NZ), 1.0, 6.0, ((1, 4), (2, 2), (3, 4)), jnp.float32)
    viscosity = jnp.clip(jnp.exp(math.log(0.15) - 2.014903 * jax.random.uniform(streams_of[2], (NX, NY, NZ), jnp.float32) ** steps_of(streams_of[2], (NX, NY, NZ), ((0, 4), (1, 2), (2, 4)), -0.2, 0.2)), 0.02, 0.15)
    records = bell_draw(streams_of[3], (FIELDS, TILES, TILE_ROWS), 1.0, 6.0, ((1, 32),), jnp.float32)
    cell_ids = with_ends(jax.random.randint(streams_of[4], (TILES, TILE_ROWS), 0, CX * CY * CZ), jax.random.fold_in(streams_of[4], 1), 0, (CX * CY * CZ) - 1).astype(jnp.int32)
    routes_keys = jax.random.split(jax.random.fold_in(streams_of[5], 1), TILES // TILES_DEV)
    routes_turns = jax.random.permutation(jax.random.fold_in(streams_of[5], 3), TILES // TILES_DEV)
    routes = jax.vmap(lambda own, number: shared_out(jax.random.fold_in(streams_of[5], 2), own, number, TILES_DEV, BLOCKS, 1, CAP, 2))(routes_keys, routes_turns).reshape((TILES, 1))
    lengths = ragged(streams_of[6], TILES, TILES * TILE_ROWS * 5 // 8, TILE_ROWS, 0).astype(jnp.int32)
    return {"density": density, "momentum_energy": momentum_energy, "viscosity": viscosity, "records": records, "cell_ids": cell_ids, "routes": routes, "lengths": lengths}


def harmonic(first_visc, second_visc):
    summed = first_visc + second_visc
    denominator = jnp.where(summed > 0, summed, 1.0)
    return 2.0 * first_visc * second_visc / denominator


def shifted(values, leading, spatial, offset):
    value_portions = [slice(None)] * leading
    for position in range(3):
        extent = values.shape[leading + position]
        if position == spatial:
            value_portions.append(slice(1 + offset, extent - 1 + offset))
        else:
            value_portions.append(slice(1, extent - 1))
    return values[tuple(value_portions)]


def viscous(field, visc):
    centre = shifted(field, 1, 0, 0)
    centre_visc = shifted(visc, 0, 0, 0)
    change = jnp.zeros_like(centre)
    for spatial in range(3):
        for offset in (1, -1):
            face_visc = harmonic(centre_visc, shifted(visc, 0, spatial, offset))
            change = change + face_visc[None] * (shifted(field, 1, spatial, offset) - centre)
    return change


def reference(density, momentum_energy, viscosity, records, cell_ids, routes, lengths):
    fluid_state = jnp.concatenate([density[None], momentum_energy], 0)
    tile_count = records.shape[1]
    row_count = records.shape[2]
    live_rows = lax.broadcasted_iota(jnp.int32, (tile_count, row_count), 1) < lengths[:, None]
    masked_values = jnp.where(live_rows[None], records, 0.0)
    device = (jnp.arange(tile_count, dtype=jnp.int32) // TILES_DEV).astype(jnp.int32)
    gore_index = device % N_GORE
    target = routes[:, 0].astype(jnp.int32)
    global_streamwise_position = (target // N_CROSS)[:, None] * CX + cell_ids // (CY * CZ)
    global_y = (target % N_CROSS)[:, None] * CY + (cell_ids // CZ) % CY
    global_z = gore_index[:, None] * CZ + cell_ids % CZ
    flat_cell = ((global_streamwise_position * NY + global_y) * NZ + global_z).astype(jnp.int32).reshape(-1)
    source_rows = masked_values[0:5].reshape(5, -1)
    source_rows = jnp.concatenate([jnp.abs(source_rows[0:1]), source_rows[1:]], 0)
    source = jnp.zeros((5, NX * NY * NZ), jnp.float32).at[:, flat_cell].add(source_rows)
    source = source.reshape(5, NX, NY, NZ)
    visc_pad = jnp.pad(viscosity, 1)
    widths = ((0, 0), (1, 1), (1, 1), (1, 1))
    middle = fluid_state + viscous(jnp.pad(fluid_state, widths), visc_pad) + source
    new_state = middle + viscous(jnp.pad(middle, widths), visc_pad)
    flat_state = new_state.reshape(5, -1)
    kinetic = flat_state[1] * flat_state[1] + flat_state[2] * flat_state[2] + flat_state[3] * flat_state[3]
    pressure = 0.4 * (flat_state[4] - 0.5 * kinetic / flat_state[0])
    face_pressure = pressure[flat_cell].reshape(tile_count, row_count)
    face_loads = masked_values[5:8] * face_pressure[None]
    return new_state, face_loads
```

```python
import jax
import jax.numpy as jnp
from jax import lax
from jax.sharding import PartitionSpec as P


SIDES = (("stream", 1), ("cross", 2), ("gore", 3))


def face_halo(block):
    padded = jnp.pad(block, ((0, 0), (1, 1), (1, 1), (1, 1)))
    for axis, dim in SIDES:
        count = lax.axis_size(axis)
        forward = [(i, i + 1) for i in range(count - 1)]
        backward = [(target, source) for source, target in forward]
        extent = block.shape[dim]
        low = lax.ppermute(lax.slice_in_dim(block, extent - 1, None, axis=dim), axis, forward)
        high = lax.ppermute(lax.slice_in_dim(block, 0, 1, axis=dim), axis, backward)
        low_at = [slice(None)] + [slice(1, -1)] * 3
        high_at = list(low_at)
        low_at[dim] = slice(0, 1)
        high_at[dim] = slice(extent + 1, extent + 2)
        padded = padded.at[tuple(low_at)].set(low).at[tuple(high_at)].set(high)
    return padded


def harmonic(first_visc, second_visc):
    summed = first_visc + second_visc
    denominator = jnp.where(summed > 0, summed, 1.0)
    return 2.0 * first_visc * second_visc / denominator


def shifted(values, leading, spatial, offset):
    value_portions = [slice(None)] * leading
    for position in range(3):
        extent = values.shape[leading + position]
        if position == spatial:
            value_portions.append(slice(1 + offset, extent - 1 + offset))
        else:
            value_portions.append(slice(1, extent - 1))
    return values[tuple(value_portions)]


def viscous(field, visc):
    centre = shifted(field, 1, 0, 0)
    centre_visc = shifted(visc, 0, 0, 0)
    change = jnp.zeros_like(centre)
    for spatial in range(3):
        for offset in (1, -1):
            face_visc = harmonic(centre_visc, shifted(visc, 0, spatial, offset))
            change = change + face_visc[None] * (shifted(field, 1, spatial, offset) - centre)
    return change


def split_high(values):
    scaled = values * jnp.float32(65537.0)
    high = scaled - (scaled - values)
    return (high, values - high)


def three_bf16(values):
    first, rest = split_high(values)
    second, third = split_high(rest)
    return tuple(part.astype(jnp.bfloat16) for part in (first, second, third))


def exact_dot(spec, values, onehot, values_first):
    stacked = jnp.stack(three_bf16(values), 0)
    left, right = spec.split("->")[0].split(",")
    output = spec.split("->")[1]
    if values_first:
        terms = jnp.einsum(
            "k" + left + "," + right + "->k" + output, stacked, onehot,
            preferred_element_type=jnp.float32,
        )
    else:
        terms = jnp.einsum(
            left + ",k" + right + "->k" + output, onehot, stacked,
            preferred_element_type=jnp.float32,
        )
    return terms[0] + terms[1] + terms[2]


def shards(density, momentum_energy, viscosity, records, cell_ids, routes, lengths):
    fluid_state = jnp.concatenate([density[None], momentum_energy], 0)
    cells_x, cells_y, vertical_cells = density.shape
    plane_count = cells_x * cells_y
    tile_count = records.shape[1]
    row_count = records.shape[2]
    blocks = lax.axis_size("stream") * lax.axis_size("cross")
    capacity = max(2, 2 * tile_count // blocks)
    slot_total = blocks * capacity
    faces = slot_total * row_count

    state_visc = face_halo(jnp.concatenate([fluid_state, viscosity[None]], 0))
    state_pad = state_visc[0:5]
    visc_pad = state_visc[5]

    live_rows = lax.broadcasted_iota(jnp.int32, (tile_count, row_count), 1) < lengths[:, None]
    masked_values = jnp.where(live_rows[None], records, 0.0)
    target = routes[:, 0]
    onehot = (target[:, None] == lax.broadcasted_iota(jnp.int32, (tile_count, blocks), 1)).astype(
        jnp.float32
    )
    lower = (
        lax.broadcasted_iota(jnp.int32, (tile_count, tile_count), 1)
        < lax.broadcasted_iota(jnp.int32, (tile_count, tile_count), 0)
    ).astype(jnp.float32)
    before = jnp.dot(
        lower, onehot, precision=lax.Precision.HIGHEST, preferred_element_type=jnp.float32
    )
    slot_rank = jnp.sum(before * onehot, axis=1).astype(jnp.int32)
    slot_index = target * capacity + slot_rank
    placement_plan = (
        slot_index[:, None] == lax.broadcasted_iota(jnp.int32, (tile_count, slot_total), 1)
    ).astype(jnp.float32)
    payload = jnp.concatenate(
        [
            jnp.abs(masked_values[0:1]),
            masked_values[1:5],
            cell_ids.astype(jnp.float32)[None],
        ],
        0,
    )
    outbound = jnp.einsum(
        "ts,ctr->csr", placement_plan, payload, precision=lax.Precision.HIGHEST
    )
    arrived = lax.all_to_all(outbound, ("stream", "cross"), split_axis=1, concat_axis=1, tiled=True)

    cells = jnp.round(arrived[5]).astype(jnp.int32).reshape(faces)
    plane = cells // vertical_cells
    depth = cells % vertical_cells
    depth_hot = (
        depth[:, None] == lax.broadcasted_iota(jnp.int32, (faces, vertical_cells), 1)
    )
    plane_rows = plane[None, :] == lax.broadcasted_iota(jnp.int32, (plane_count, faces), 0)
    spread = jnp.where(plane_rows[None], arrived[0:5].reshape(5, 1, faces), 0.0)
    source = jnp.einsum(
        "cpf,fd->cpd", spread, depth_hot.astype(jnp.float32), precision=lax.Precision.HIGHEST
    )
    source = source.reshape(5, cells_x, cells_y, vertical_cells)

    middle = shifted(state_pad, 1, 0, 0) + viscous(state_pad, visc_pad) + source
    middle_pad = face_halo(middle)
    new_state = middle + viscous(middle_pad, visc_pad)

    flat_state = new_state.reshape(5, plane_count, vertical_cells)
    kinetic = (
        flat_state[1] * flat_state[1]
        + flat_state[2] * flat_state[2]
        + flat_state[3] * flat_state[3]
    )
    pressure = 0.4 * (flat_state[4] - 0.5 * kinetic / flat_state[0])
    picked = exact_dot("fd,dp->fp", pressure.T, depth_hot.astype(jnp.bfloat16), False)
    plane_cols = plane[:, None] == lax.broadcasted_iota(jnp.int32, (faces, plane_count), 1)
    face_pressure = jnp.sum(jnp.where(plane_cols, picked, 0.0), axis=1)
    returned = lax.all_to_all(
        face_pressure.reshape(1, slot_total, row_count),
        ("stream", "cross"),
        split_axis=1,
        concat_axis=1,
        tiled=True,
    )
    home_pressure = jnp.einsum(
        "ts,sr->tr", placement_plan, returned[0], precision=lax.Precision.HIGHEST
    )
    face_loads = masked_values[5:8] * home_pressure[None]
    return (new_state, face_loads)


def solution(mesh):
    placed = (
        P("stream", "cross", "gore"),
        P(None, "stream", "cross", "gore"),
        P("stream", "cross", "gore"),
        P(None, ("stream", "cross", "gore"), None),
        P(("stream", "cross", "gore"), None),
        P(("stream", "cross", "gore"), None),
        P(("stream", "cross", "gore")),
    )
    return jax.shard_map(
        shards,
        mesh=mesh,
        in_specs=placed,
        out_specs=(P(None, "stream", "cross", "gore"), P(None, ("stream", "cross", "gore"), None)),
        check_vma=False,
    )
```

```python
import jax
import jax.numpy as jnp
from jax import lax
from jax.sharding import PartitionSpec as P


SIDES = (("stream", 1), ("cross", 2), ("gore", 3))


def face_halo(block):
    wide = block
    for axis, dim in SIDES:
        count = lax.axis_size(axis)
        forward = [(i, i + 1) for i in range(count - 1)]
        backward = [(target, source) for source, target in forward]
        extent = block.shape[dim]
        low = lax.ppermute(lax.slice_in_dim(block, extent - 1, None, axis=dim), axis, forward)
        high = lax.ppermute(lax.slice_in_dim(block, 0, 1, axis=dim), axis, backward)
        widths = [(0, 0)] + [(1, 1) if d < dim else (0, 0) for d in range(1, 4)]
        wide = jnp.concatenate([jnp.pad(low, widths), wide, jnp.pad(high, widths)], axis=dim)
    return wide


def harmonic(first_visc, second_visc):
    summed = first_visc + second_visc
    denominator = jnp.where(summed > 0, summed, 1.0)
    return 2.0 * first_visc * second_visc / denominator


def shifted(values, leading, spatial, offset):
    value_portions = [slice(None)] * leading
    for position in range(3):
        extent = values.shape[leading + position]
        if position == spatial:
            value_portions.append(slice(1 + offset, extent - 1 + offset))
        else:
            value_portions.append(slice(1, extent - 1))
    return values[tuple(value_portions)]


def viscous(field, visc):
    centre = shifted(field, 1, 0, 0)
    centre_visc = shifted(visc, 0, 0, 0)
    change = jnp.zeros_like(centre)
    for spatial in range(3):
        for offset in (1, -1):
            face_visc = harmonic(centre_visc, shifted(visc, 0, spatial, offset))
            change = change + face_visc[None] * (shifted(field, 1, spatial, offset) - centre)
    return change


def split_high(values):
    scaled = values * jnp.float32(65537.0)
    high = scaled - (scaled - values)
    return (high, values - high)


def three_bf16(values):
    first, rest = split_high(values)
    second, third = split_high(rest)
    return tuple(part.astype(jnp.bfloat16) for part in (first, second, third))


def exact_dot(spec, values, onehot, values_first):
    stacked = jnp.stack(three_bf16(values), 0)
    left, right = spec.split("->")[0].split(",")
    output = spec.split("->")[1]
    if values_first:
        terms = jnp.einsum(
            "k" + left + "," + right + "->k" + output, stacked, onehot,
            preferred_element_type=jnp.float32,
        )
    else:
        terms = jnp.einsum(
            left + ",k" + right + "->k" + output, onehot, stacked,
            preferred_element_type=jnp.float32,
        )
    return terms[0] + terms[1] + terms[2]


def shards(density, momentum_energy, viscosity, records, cell_ids, routes, lengths):
    fluid_state = jnp.concatenate([density[None], momentum_energy], 0)
    cells_x, cells_y, vertical_cells = density.shape
    plane_count = cells_x * cells_y
    tile_count = records.shape[1]
    row_count = records.shape[2]
    blocks = lax.axis_size("stream") * lax.axis_size("cross")
    capacity = max(2, 2 * tile_count // blocks)
    slot_total = blocks * capacity
    faces = slot_total * row_count

    state_visc = face_halo(jnp.concatenate([fluid_state, viscosity[None]], 0))
    state_pad = state_visc[0:5]
    visc_pad = state_visc[5]

    live_rows = lax.broadcasted_iota(jnp.int32, (tile_count, row_count), 1) < lengths[:, None]
    masked_values = jnp.where(live_rows[None], records, 0.0)
    target = routes[:, 0]
    onehot = (target[:, None] == lax.broadcasted_iota(jnp.int32, (tile_count, blocks), 1)).astype(
        jnp.float32
    )
    lower = (
        lax.broadcasted_iota(jnp.int32, (tile_count, tile_count), 1)
        < lax.broadcasted_iota(jnp.int32, (tile_count, tile_count), 0)
    ).astype(jnp.float32)
    before = jnp.dot(
        lower, onehot, precision=lax.Precision.HIGHEST, preferred_element_type=jnp.float32
    )
    slot_rank = jnp.sum(before * onehot, axis=1).astype(jnp.int32)
    slot_index = target * capacity + slot_rank
    placement_plan = (
        slot_index[:, None] == lax.broadcasted_iota(jnp.int32, (tile_count, slot_total), 1)
    ).astype(jnp.float32)
    payload = jnp.concatenate(
        [
            jnp.abs(masked_values[0:1]),
            masked_values[1:5],
            cell_ids.astype(jnp.float32)[None],
        ],
        0,
    )
    outbound = jnp.einsum(
        "ts,ctr->csr", placement_plan, payload, precision=lax.Precision.HIGHEST
    )
    arrived = lax.all_to_all(outbound, ("stream", "cross"), split_axis=1, concat_axis=1, tiled=True)

    cells = jnp.round(arrived[5]).astype(jnp.int32).reshape(faces)
    plane = cells // vertical_cells
    depth = cells % vertical_cells
    depth_hot = (
        depth[:, None] == lax.broadcasted_iota(jnp.int32, (faces, vertical_cells), 1)
    )
    plane_rows = plane[None, :] == lax.broadcasted_iota(jnp.int32, (plane_count, faces), 0)
    spread = jnp.where(plane_rows[None], arrived[0:5].reshape(5, 1, faces), 0.0)
    source = jnp.einsum(
        "cpf,fd->cpd", spread, depth_hot.astype(jnp.float32), precision=lax.Precision.HIGHEST
    )
    source = source.reshape(5, cells_x, cells_y, vertical_cells)

    middle = shifted(state_pad, 1, 0, 0) + viscous(state_pad, visc_pad) + source
    middle_pad = face_halo(middle)
    new_state = middle + viscous(middle_pad, visc_pad)

    flat_state = new_state.reshape(5, plane_count, vertical_cells)
    kinetic = (
        flat_state[1] * flat_state[1]
        + flat_state[2] * flat_state[2]
        + flat_state[3] * flat_state[3]
    )
    pressure = 0.4 * (flat_state[4] - 0.5 * kinetic / flat_state[0])
    picked = exact_dot("fd,dp->fp", pressure.T, depth_hot.astype(jnp.bfloat16), False)
    plane_cols = plane[:, None] == lax.broadcasted_iota(jnp.int32, (faces, plane_count), 1)
    face_pressure = jnp.sum(jnp.where(plane_cols, picked, 0.0), axis=1)
    returned = lax.all_to_all(
        face_pressure.reshape(1, slot_total, row_count),
        ("stream", "cross"),
        split_axis=1,
        concat_axis=1,
        tiled=True,
    )
    home_pressure = jnp.einsum(
        "ts,sr->tr", placement_plan, returned[0], precision=lax.Precision.HIGHEST
    )
    face_loads = masked_values[5:8] * home_pressure[None]
    return (new_state, face_loads)


def solution(mesh):
    placed = (
        P("stream", "cross", "gore"),
        P(None, "stream", "cross", "gore"),
        P("stream", "cross", "gore"),
        P(None, ("stream", "cross", "gore"), None),
        P(("stream", "cross", "gore"), None),
        P(("stream", "cross", "gore"), None),
        P(("stream", "cross", "gore")),
    )
    return jax.shard_map(
        shards,
        mesh=mesh,
        in_specs=placed,
        out_specs=(P(None, "stream", "cross", "gore"), P(None, ("stream", "cross", "gore"), None)),
        check_vma=False,
    )
```

```python
import jax
import jax.numpy as jnp
from jax import lax
from jax.sharding import PartitionSpec as P


SIDES = (("stream", 1), ("cross", 2), ("gore", 3))


def face_halo(block):
    wide = block
    for axis, dim in SIDES:
        count = lax.axis_size(axis)
        index = lax.axis_index(axis)
        odd = index % 2 == 1
        extent = block.shape[dim]
        last = lax.slice_in_dim(block, extent - 1, None, axis=dim)
        first = lax.slice_in_dim(block, 0, 1, axis=dim)
        pairs_a = [(i, i ^ 1) for i in range(count) if (i ^ 1) < count]
        pairs_b = [(i, j) for i in range(1, count) for j in (i - 1, i + 1) if j >= 1 and j < count and (min(i, j) % 2 == 1)]
        from_a = lax.ppermute(jnp.where(odd, first, last), axis, pairs_a)
        if pairs_b:
            from_b = lax.ppermute(jnp.where(odd, last, first), axis, pairs_b)
        else:
            from_b = jnp.zeros_like(from_a)
        low = jnp.where(odd, from_a, from_b)
        high = jnp.where(odd, from_b, from_a)
        widths = [(0, 0)] + [(1, 1) if d < dim else (0, 0) for d in range(1, 4)]
        wide = jnp.concatenate([jnp.pad(low, widths), wide, jnp.pad(high, widths)], axis=dim)
    return wide


def harmonic(first_visc, second_visc):
    summed = first_visc + second_visc
    denominator = jnp.where(summed > 0, summed, 1.0)
    return 2.0 * first_visc * second_visc / denominator


def shifted(values, leading, spatial, offset):
    value_portions = [slice(None)] * leading
    for position in range(3):
        extent = values.shape[leading + position]
        if position == spatial:
            value_portions.append(slice(1 + offset, extent - 1 + offset))
        else:
            value_portions.append(slice(1, extent - 1))
    return values[tuple(value_portions)]


def viscous(field, visc):
    centre = shifted(field, 1, 0, 0)
    centre_visc = shifted(visc, 0, 0, 0)
    change = jnp.zeros_like(centre)
    for spatial in range(3):
        for offset in (1, -1):
            face_visc = harmonic(centre_visc, shifted(visc, 0, spatial, offset))
            change = change + face_visc[None] * (shifted(field, 1, spatial, offset) - centre)
    return change


def split_high(values):
    scaled = values * jnp.float32(65537.0)
    high = scaled - (scaled - values)
    return (high, values - high)


def three_bf16(values):
    first, rest = split_high(values)
    second, third = split_high(rest)
    return tuple(part.astype(jnp.bfloat16) for part in (first, second, third))


def exact_dot(spec, values, onehot, values_first):
    stacked = jnp.stack(three_bf16(values), 0)
    left, right = spec.split("->")[0].split(",")
    output = spec.split("->")[1]
    if values_first:
        terms = jnp.einsum(
            "k" + left + "," + right + "->k" + output, stacked, onehot,
            preferred_element_type=jnp.float32,
        )
    else:
        terms = jnp.einsum(
            left + ",k" + right + "->k" + output, onehot, stacked,
            preferred_element_type=jnp.float32,
        )
    return terms[0] + terms[1] + terms[2]


def shards(density, momentum_energy, viscosity, records, cell_ids, routes, lengths):
    fluid_state = jnp.concatenate([density[None], momentum_energy], 0)
    cells_x, cells_y, vertical_cells = density.shape
    plane_count = cells_x * cells_y
    tile_count = records.shape[1]
    row_count = records.shape[2]
    blocks = lax.axis_size("stream") * lax.axis_size("cross")
    capacity = max(2, 2 * tile_count // blocks)
    slot_total = blocks * capacity

    state_visc = face_halo(jnp.concatenate([fluid_state, viscosity[None]], 0))
    state_pad = state_visc[0:5]
    visc_pad = state_visc[5]

    live_rows = lax.broadcasted_iota(jnp.int32, (tile_count, row_count), 1) < lengths[:, None]
    masked_values = jnp.where(live_rows[None], records, 0.0)
    target = routes[:, 0]
    onehot = (target[:, None] == lax.broadcasted_iota(jnp.int32, (tile_count, blocks), 1)).astype(
        jnp.float32
    )
    lower = (
        lax.broadcasted_iota(jnp.int32, (tile_count, tile_count), 1)
        < lax.broadcasted_iota(jnp.int32, (tile_count, tile_count), 0)
    ).astype(jnp.float32)
    before = jnp.dot(
        lower, onehot, precision=lax.Precision.HIGHEST, preferred_element_type=jnp.float32
    )
    slot_rank = jnp.sum(before * onehot, axis=1).astype(jnp.int32)
    slot_index = target * capacity + slot_rank
    placement_plan = (
        slot_index[:, None] == lax.broadcasted_iota(jnp.int32, (tile_count, slot_total), 1)
    ).astype(jnp.float32)
    payload = jnp.concatenate(
        [
            jnp.abs(masked_values[0:1]),
            masked_values[1:5],
            cell_ids.astype(jnp.float32)[None],
        ],
        0,
    )
    outbound = jnp.einsum(
        "ts,ctr->scr", placement_plan, payload, precision=lax.Precision.HIGHEST
    )
    arrived = lax.all_to_all(outbound, ("stream", "cross"), split_axis=0, concat_axis=0, tiled=True)

    cells = jnp.round(arrived[:, 5]).astype(jnp.int32)
    plane = cells // vertical_cells
    depth = cells % vertical_cells
    depth_hot = (
        depth[:, :, None]
        == lax.broadcasted_iota(jnp.int32, (slot_total, row_count, vertical_cells), 2)
    )
    plane_rows = plane[None] == lax.broadcasted_iota(
        jnp.int32, (plane_count, slot_total, row_count), 0
    )
    spread = jnp.where(plane_rows[None], arrived[:, 0:5].transpose(1, 0, 2)[:, None], 0.0)
    source = jnp.einsum(
        "cpsr,srd->cpd", spread, depth_hot.astype(jnp.float32), precision=lax.Precision.HIGHEST
    )
    source = source.reshape(5, cells_x, cells_y, vertical_cells)

    middle = shifted(state_pad, 1, 0, 0) + viscous(state_pad, visc_pad) + source
    middle_pad = face_halo(middle)
    new_state = middle + viscous(middle_pad, visc_pad)

    flat_state = new_state.reshape(5, plane_count, vertical_cells)
    kinetic = (
        flat_state[1] * flat_state[1]
        + flat_state[2] * flat_state[2]
        + flat_state[3] * flat_state[3]
    )
    pressure = 0.4 * (flat_state[4] - 0.5 * kinetic / flat_state[0])
    picked = exact_dot("srd,dp->srp", pressure.T, depth_hot.astype(jnp.bfloat16), False)
    plane_cols = plane[:, :, None] == lax.broadcasted_iota(
        jnp.int32, (slot_total, row_count, plane_count), 2
    )
    face_pressure = jnp.sum(jnp.where(plane_cols, picked, 0.0), axis=2)
    returned = lax.all_to_all(
        face_pressure.reshape(1, slot_total, row_count),
        ("stream", "cross"),
        split_axis=1,
        concat_axis=1,
        tiled=True,
    )
    home_pressure = jnp.einsum(
        "ts,sr->tr", placement_plan, returned[0], precision=lax.Precision.HIGHEST
    )
    face_loads = masked_values[5:8] * home_pressure[None]
    return (new_state, face_loads)


def solution(mesh):
    placed = (
        P("stream", "cross", "gore"),
        P(None, "stream", "cross", "gore"),
        P("stream", "cross", "gore"),
        P(None, ("stream", "cross", "gore"), None),
        P(("stream", "cross", "gore"), None),
        P(("stream", "cross", "gore"), None),
        P(("stream", "cross", "gore")),
    )
    return jax.shard_map(
        shards,
        mesh=mesh,
        in_specs=placed,
        out_specs=(P(None, "stream", "cross", "gore"), P(None, ("stream", "cross", "gore"), None)),
        check_vma=False,
    )
```

```python
import jax
import jax.numpy as jnp
from jax import lax
from jax.sharding import PartitionSpec as P


SIDES = (("stream", 1), ("cross", 2), ("gore", 3))


def face_halo(block):
    wide = block
    for axis, dim in SIDES:
        count = lax.axis_size(axis)
        index = lax.axis_index(axis)
        odd = index % 2 == 1
        extent = block.shape[dim]
        last = lax.slice_in_dim(block, extent - 1, None, axis=dim)
        first = lax.slice_in_dim(block, 0, 1, axis=dim)
        pairs_a = [(i, i ^ 1) for i in range(count) if (i ^ 1) < count]
        pairs_b = [(i, j) for i in range(1, count) for j in (i - 1, i + 1) if j >= 1 and j < count and (min(i, j) % 2 == 1)]
        from_a = lax.ppermute(jnp.where(odd, first, last), axis, pairs_a)
        if pairs_b:
            from_b = lax.ppermute(jnp.where(odd, last, first), axis, pairs_b)
        else:
            from_b = jnp.zeros_like(from_a)
        low = jnp.where(odd, from_a, from_b)
        high = jnp.where(odd, from_b, from_a)
        widths = [(0, 0)] + [(1, 1) if d < dim else (0, 0) for d in range(1, 4)]
        wide = jnp.concatenate([jnp.pad(low, widths), wide, jnp.pad(high, widths)], axis=dim)
    return wide


def harmonic(first_visc, second_visc):
    summed = first_visc + second_visc
    denominator = jnp.where(summed > 0, summed, 1.0)
    return 2.0 * first_visc * second_visc / denominator


def shifted(values, leading, spatial, offset):
    value_portions = [slice(None)] * leading
    for position in range(3):
        extent = values.shape[leading + position]
        if position == spatial:
            value_portions.append(slice(1 + offset, extent - 1 + offset))
        else:
            value_portions.append(slice(1, extent - 1))
    return values[tuple(value_portions)]


def viscous(field, visc):
    centre = shifted(field, 1, 0, 0)
    centre_visc = shifted(visc, 0, 0, 0)
    change = jnp.zeros_like(centre)
    for spatial in range(3):
        for offset in (1, -1):
            face_visc = harmonic(centre_visc, shifted(visc, 0, spatial, offset))
            change = change + face_visc[None] * (shifted(field, 1, spatial, offset) - centre)
    return change


def split_high(values):
    scaled = values * jnp.float32(65537.0)
    high = scaled - (scaled - values)
    return (high, values - high)


def three_bf16(values):
    first, rest = split_high(values)
    second, third = split_high(rest)
    return tuple(part.astype(jnp.bfloat16) for part in (first, second, third))


def exact_dot(spec, values, onehot, values_first):
    stacked = jnp.stack(three_bf16(values), 0)
    left, right = spec.split("->")[0].split(",")
    output = spec.split("->")[1]
    if values_first:
        terms = jnp.einsum(
            "k" + left + "," + right + "->k" + output, stacked, onehot,
            preferred_element_type=jnp.float32,
        )
    else:
        terms = jnp.einsum(
            left + ",k" + right + "->k" + output, onehot, stacked,
            preferred_element_type=jnp.float32,
        )
    return terms[0] + terms[1] + terms[2]


def shards(density, momentum_energy, viscosity, records, cell_ids, routes, lengths):
    fluid_state = jnp.concatenate([density[None], momentum_energy], 0)
    cells_x, cells_y, vertical_cells = density.shape
    plane_count = cells_x * cells_y
    tile_count = records.shape[1]
    row_count = records.shape[2]
    blocks = lax.axis_size("stream") * lax.axis_size("cross")
    capacity = max(2, 2 * tile_count // blocks)
    slot_total = blocks * capacity
    faces = slot_total * row_count

    live_rows = lax.broadcasted_iota(jnp.int32, (tile_count, row_count), 1) < lengths[:, None]
    masked_values = jnp.where(live_rows[None], records, 0.0)
    target = routes[:, 0]
    onehot = (target[:, None] == lax.broadcasted_iota(jnp.int32, (tile_count, blocks), 1)).astype(
        jnp.float32
    )
    lower = (
        lax.broadcasted_iota(jnp.int32, (tile_count, tile_count), 1)
        < lax.broadcasted_iota(jnp.int32, (tile_count, tile_count), 0)
    ).astype(jnp.float32)
    before = jnp.dot(
        lower, onehot, precision=lax.Precision.HIGHEST, preferred_element_type=jnp.float32
    )
    slot_rank = jnp.sum(before * onehot, axis=1).astype(jnp.int32)
    slot_index = target * capacity + slot_rank
    placement_plan = (
        slot_index[:, None] == lax.broadcasted_iota(jnp.int32, (tile_count, slot_total), 1)
    ).astype(jnp.float32)
    payload = jnp.concatenate(
        [
            jnp.abs(masked_values[0:1]),
            masked_values[1:5],
            cell_ids.astype(jnp.float32)[None],
        ],
        0,
    )
    outbound = jnp.einsum(
        "ts,ctr->csr", placement_plan, payload, precision=lax.Precision.HIGHEST
    )
    arrived = lax.all_to_all(outbound, ("stream", "cross"), split_axis=1, concat_axis=1, tiled=True)
    outbound, state_and_visc = lax.optimization_barrier(
        (outbound, jnp.concatenate([fluid_state, viscosity[None]], 0))
    )
    state_visc = face_halo(state_and_visc)
    state_pad = state_visc[0:5]
    visc_pad = state_visc[5]

    cells = jnp.round(arrived[5]).astype(jnp.int32).reshape(faces)
    plane = cells // vertical_cells
    depth = cells % vertical_cells
    depth_hot = (
        depth[:, None] == lax.broadcasted_iota(jnp.int32, (faces, vertical_cells), 1)
    )
    plane_rows = plane[None, :] == lax.broadcasted_iota(jnp.int32, (plane_count, faces), 0)
    spread = jnp.where(plane_rows[None], arrived[0:5].reshape(5, 1, faces), 0.0)
    source = jnp.einsum(
        "cpf,fd->cpd", spread, depth_hot.astype(jnp.float32), precision=lax.Precision.HIGHEST
    )
    source = source.reshape(5, cells_x, cells_y, vertical_cells)

    middle = shifted(state_pad, 1, 0, 0) + viscous(state_pad, visc_pad) + source
    middle_pad = face_halo(middle)
    new_state = middle + viscous(middle_pad, visc_pad)

    flat_state = new_state.reshape(5, plane_count, vertical_cells)
    kinetic = (
        flat_state[1] * flat_state[1]
        + flat_state[2] * flat_state[2]
        + flat_state[3] * flat_state[3]
    )
    pressure = 0.4 * (flat_state[4] - 0.5 * kinetic / flat_state[0])
    picked = exact_dot("fd,dp->fp", pressure.T, depth_hot.astype(jnp.bfloat16), False)
    plane_cols = plane[:, None] == lax.broadcasted_iota(jnp.int32, (faces, plane_count), 1)
    face_pressure = jnp.sum(jnp.where(plane_cols, picked, 0.0), axis=1)
    returned = lax.all_to_all(
        face_pressure.reshape(1, slot_total, row_count),
        ("stream", "cross"),
        split_axis=1,
        concat_axis=1,
        tiled=True,
    )
    home_pressure = jnp.einsum(
        "ts,sr->tr", placement_plan, returned[0], precision=lax.Precision.HIGHEST
    )
    face_loads = masked_values[5:8] * home_pressure[None]
    return (new_state, face_loads)


def solution(mesh):
    placed = (
        P("stream", "cross", "gore"),
        P(None, "stream", "cross", "gore"),
        P("stream", "cross", "gore"),
        P(None, ("stream", "cross", "gore"), None),
        P(("stream", "cross", "gore"), None),
        P(("stream", "cross", "gore"), None),
        P(("stream", "cross", "gore")),
    )
    return jax.shard_map(
        shards,
        mesh=mesh,
        in_specs=placed,
        out_specs=(P(None, "stream", "cross", "gore"), P(None, ("stream", "cross", "gore"), None)),
        check_vma=False,
    )
```

```python
import jax
import jax.numpy as jnp
from jax import lax
from jax.sharding import PartitionSpec as P


SIDES = (("stream", 1), ("cross", 2), ("gore", 3))


def face_halo(block):
    wide = block
    for axis, dim in SIDES:
        count = lax.axis_size(axis)
        index = lax.axis_index(axis)
        odd = index % 2 == 1
        extent = block.shape[dim]
        last = lax.slice_in_dim(block, extent - 1, None, axis=dim)
        first = lax.slice_in_dim(block, 0, 1, axis=dim)
        pairs_a = [(i, i ^ 1) for i in range(count) if (i ^ 1) < count]
        pairs_b = [(i, j) for i in range(1, count) for j in (i - 1, i + 1) if j >= 1 and j < count and (min(i, j) % 2 == 1)]
        from_a = lax.ppermute(jnp.where(odd, first, last), axis, pairs_a)
        if pairs_b:
            from_b = lax.ppermute(jnp.where(odd, last, first), axis, pairs_b)
        else:
            from_b = jnp.zeros_like(from_a)
        low = jnp.where(odd, from_a, from_b)
        high = jnp.where(odd, from_b, from_a)
        widths = [(0, 0)] + [(1, 1) if d < dim else (0, 0) for d in range(1, 4)]
        wide = jnp.concatenate([jnp.pad(low, widths), wide, jnp.pad(high, widths)], axis=dim)
    return wide


def harmonic(first_visc, second_visc):
    summed = first_visc + second_visc
    denominator = jnp.where(summed > 0, summed, 1.0)
    return 2.0 * first_visc * second_visc / denominator


def shifted(values, leading, spatial, offset):
    value_portions = [slice(None)] * leading
    for position in range(3):
        extent = values.shape[leading + position]
        if position == spatial:
            value_portions.append(slice(1 + offset, extent - 1 + offset))
        else:
            value_portions.append(slice(1, extent - 1))
    return values[tuple(value_portions)]


def viscous(field, visc):
    centre = shifted(field, 1, 0, 0)
    centre_visc = shifted(visc, 0, 0, 0)
    change = jnp.zeros_like(centre)
    for spatial in range(3):
        for offset in (1, -1):
            face_visc = harmonic(centre_visc, shifted(visc, 0, spatial, offset))
            change = change + face_visc[None] * (shifted(field, 1, spatial, offset) - centre)
    return change


def split_high(values):
    scaled = values * jnp.float32(65537.0)
    high = scaled - (scaled - values)
    return (high, values - high)


def three_bf16(values):
    first, rest = split_high(values)
    second, third = split_high(rest)
    return tuple(part.astype(jnp.bfloat16) for part in (first, second, third))


def exact_dot(spec, values, onehot, values_first):
    stacked = jnp.stack(three_bf16(values), 0)
    left, right = spec.split("->")[0].split(",")
    output = spec.split("->")[1]
    if values_first:
        terms = jnp.einsum(
            "k" + left + "," + right + "->k" + output, stacked, onehot,
            preferred_element_type=jnp.float32,
        )
    else:
        terms = jnp.einsum(
            left + ",k" + right + "->k" + output, onehot, stacked,
            preferred_element_type=jnp.float32,
        )
    return terms[0] + terms[1] + terms[2]


def shards(density, momentum_energy, viscosity, records, cell_ids, routes, lengths):
    fluid_state = jnp.concatenate([density[None], momentum_energy], 0)
    cells_x, cells_y, vertical_cells = density.shape
    plane_count = cells_x * cells_y
    tile_count = records.shape[1]
    row_count = records.shape[2]
    blocks = lax.axis_size("stream") * lax.axis_size("cross")
    capacity = max(2, 2 * tile_count // blocks)
    slot_total = blocks * capacity
    faces = slot_total * row_count

    live_rows = lax.broadcasted_iota(jnp.int32, (tile_count, row_count), 1) < lengths[:, None]
    masked_values = jnp.where(live_rows[None], records, 0.0)
    target = routes[:, 0]
    onehot = (target[:, None] == lax.broadcasted_iota(jnp.int32, (tile_count, blocks), 1)).astype(
        jnp.float32
    )
    lower = (
        lax.broadcasted_iota(jnp.int32, (tile_count, tile_count), 1)
        < lax.broadcasted_iota(jnp.int32, (tile_count, tile_count), 0)
    ).astype(jnp.float32)
    before = jnp.dot(
        lower, onehot, precision=lax.Precision.HIGHEST, preferred_element_type=jnp.float32
    )
    slot_rank = jnp.sum(before * onehot, axis=1).astype(jnp.int32)
    slot_index = target * capacity + slot_rank
    placement_plan = (
        slot_index[:, None] == lax.broadcasted_iota(jnp.int32, (tile_count, slot_total), 1)
    ).astype(jnp.float32)
    payload = jnp.concatenate(
        [
            jnp.abs(masked_values[0:1]),
            masked_values[1:5],
            cell_ids.astype(jnp.float32)[None],
        ],
        0,
    )
    outbound = jnp.einsum(
        "ts,ctr->csr", placement_plan, payload, precision=lax.Precision.HIGHEST
    )
    arrived = lax.all_to_all(outbound, ("stream", "cross"), split_axis=1, concat_axis=1, tiled=True)
    outbound, state_and_visc = lax.optimization_barrier(
        (outbound, jnp.concatenate([fluid_state, viscosity[None]], 0))
    )
    state_visc = face_halo(state_and_visc)
    state_pad = state_visc[0:5]
    visc_pad = state_visc[5]

    cells = jnp.round(arrived[5]).astype(jnp.int32).reshape(faces)
    plane = cells // vertical_cells
    depth = cells % vertical_cells
    depth_hot = (
        depth[:, None] == lax.broadcasted_iota(jnp.int32, (faces, vertical_cells), 1)
    )
    plane_rows = plane[None, :] == lax.broadcasted_iota(jnp.int32, (plane_count, faces), 0)
    spread = jnp.where(plane_rows[None], arrived[0:5].reshape(5, 1, faces), 0.0)
    source = jnp.einsum(
        "cpf,fd->cpd", spread, depth_hot.astype(jnp.float32), precision=lax.Precision.HIGHEST
    )
    source = source.reshape(5, cells_x, cells_y, vertical_cells)

    middle = shifted(state_pad, 1, 0, 0) + viscous(state_pad, visc_pad) + source
    middle_pad = face_halo(middle)
    new_state = middle + viscous(middle_pad, visc_pad)

    flat_state = new_state.reshape(5, plane_count, vertical_cells)
    kinetic = (
        flat_state[1] * flat_state[1]
        + flat_state[2] * flat_state[2]
        + flat_state[3] * flat_state[3]
    )
    pressure = 0.4 * (flat_state[4] - 0.5 * kinetic / flat_state[0])
    pressure_all = lax.all_gather(pressure, ("stream", "cross"))
    home_depth = (
        (cell_ids % vertical_cells)[:, :, None]
        == lax.broadcasted_iota(jnp.int32, (tile_count, row_count, vertical_cells), 2)
    ).astype(jnp.bfloat16)
    home_plane = cell_ids // vertical_cells
    if blocks * plane_count <= 512:
        table = pressure_all.reshape(blocks * plane_count, vertical_cells)
        key = target[:, None] * plane_count + home_plane
        picked = exact_dot("trd,dq->trq", table.T, home_depth, False)
        chosen = key[:, :, None] == lax.broadcasted_iota(
            jnp.int32, (tile_count, row_count, blocks * plane_count), 2
        )
    else:
        tile_table = jnp.einsum(
            "tb,bq->tq",
            onehot,
            pressure_all.reshape(blocks, plane_count * vertical_cells),
            precision=lax.Precision.HIGHEST,
        ).reshape(tile_count, plane_count, vertical_cells)
        picked = exact_dot("trd,tpd->trp", tile_table, home_depth, False)
        chosen = home_plane[:, :, None] == lax.broadcasted_iota(
            jnp.int32, (tile_count, row_count, plane_count), 2
        )
    home_pressure = jnp.sum(jnp.where(chosen, picked, 0.0), axis=2)
    face_loads = masked_values[5:8] * home_pressure[None]
    return (new_state, face_loads)


def solution(mesh):
    placed = (
        P("stream", "cross", "gore"),
        P(None, "stream", "cross", "gore"),
        P("stream", "cross", "gore"),
        P(None, ("stream", "cross", "gore"), None),
        P(("stream", "cross", "gore"), None),
        P(("stream", "cross", "gore"), None),
        P(("stream", "cross", "gore")),
    )
    return jax.shard_map(
        shards,
        mesh=mesh,
        in_specs=placed,
        out_specs=(P(None, "stream", "cross", "gore"), P(None, ("stream", "cross", "gore"), None)),
        check_vma=False,
    )
```

```python
import jax
import jax.numpy as jnp
from jax import lax
from jax.sharding import PartitionSpec as P


SIDES = (("stream", 1), ("cross", 2), ("gore", 3))


def face_halo(block):
    wide = block
    for axis, dim in SIDES:
        count = lax.axis_size(axis)
        index = lax.axis_index(axis)
        odd = index % 2 == 1
        extent = block.shape[dim]
        last = lax.slice_in_dim(block, extent - 1, None, axis=dim)
        first = lax.slice_in_dim(block, 0, 1, axis=dim)
        pairs_a = [(i, i ^ 1) for i in range(count) if (i ^ 1) < count]
        pairs_b = [(i, j) for i in range(1, count) for j in (i - 1, i + 1) if j >= 1 and j < count and (min(i, j) % 2 == 1)]
        from_a = lax.ppermute(jnp.where(odd, first, last), axis, pairs_a)
        if pairs_b:
            from_b = lax.ppermute(jnp.where(odd, last, first), axis, pairs_b)
        else:
            from_b = jnp.zeros_like(from_a)
        low = jnp.where(odd, from_a, from_b)
        high = jnp.where(odd, from_b, from_a)
        widths = [(0, 0)] + [(1, 1) if d < dim else (0, 0) for d in range(1, 4)]
        wide = jnp.concatenate([jnp.pad(low, widths), wide, jnp.pad(high, widths)], axis=dim)
    return wide


def harmonic(first_visc, second_visc):
    summed = first_visc + second_visc
    denominator = jnp.where(summed > 0, summed, 1.0)
    return 2.0 * first_visc * second_visc / denominator


def shifted(values, leading, spatial, offset):
    value_portions = [slice(None)] * leading
    for position in range(3):
        extent = values.shape[leading + position]
        if position == spatial:
            value_portions.append(slice(1 + offset, extent - 1 + offset))
        else:
            value_portions.append(slice(1, extent - 1))
    return values[tuple(value_portions)]


def viscous(field, visc):
    centre = shifted(field, 1, 0, 0)
    centre_visc = shifted(visc, 0, 0, 0)
    change = jnp.zeros_like(centre)
    for spatial in range(3):
        for offset in (1, -1):
            face_visc = harmonic(centre_visc, shifted(visc, 0, spatial, offset))
            change = change + face_visc[None] * (shifted(field, 1, spatial, offset) - centre)
    return change


def split_high(values):
    scaled = values * jnp.float32(65537.0)
    high = scaled - (scaled - values)
    return (high, values - high)


def three_bf16(values):
    first, rest = split_high(values)
    second, third = split_high(rest)
    return tuple(part.astype(jnp.bfloat16) for part in (first, second, third))


def exact_dot(spec, values, onehot, values_first):
    stacked = jnp.stack(three_bf16(values), 0)
    left, right = spec.split("->")[0].split(",")
    output = spec.split("->")[1]
    if values_first:
        terms = jnp.einsum(
            "k" + left + "," + right + "->k" + output, stacked, onehot,
            preferred_element_type=jnp.float32,
        )
    else:
        terms = jnp.einsum(
            left + ",k" + right + "->k" + output, onehot, stacked,
            preferred_element_type=jnp.float32,
        )
    return terms[0] + terms[1] + terms[2]


def shards(density, momentum_energy, viscosity, records, cell_ids, routes, lengths):
    fluid_state = jnp.concatenate([density[None], momentum_energy], 0)
    cells_x, cells_y, vertical_cells = density.shape
    plane_count = cells_x * cells_y
    tile_count = records.shape[1]
    row_count = records.shape[2]
    blocks = lax.axis_size("stream") * lax.axis_size("cross")
    capacity = max(2, 2 * tile_count // blocks)
    slot_total = blocks * capacity
    faces = slot_total * row_count

    live_rows = lax.broadcasted_iota(jnp.int32, (tile_count, row_count), 1) < lengths[:, None]
    target = routes[:, 0]
    onehot = (target[:, None] == lax.broadcasted_iota(jnp.int32, (tile_count, blocks), 1)).astype(
        jnp.float32
    )
    lower = (
        lax.broadcasted_iota(jnp.int32, (tile_count, tile_count), 1)
        < lax.broadcasted_iota(jnp.int32, (tile_count, tile_count), 0)
    ).astype(jnp.float32)
    before = jnp.dot(
        lower, onehot, precision=lax.Precision.HIGHEST, preferred_element_type=jnp.float32
    )
    slot_rank = jnp.sum(before * onehot, axis=1).astype(jnp.int32)
    slot_index = target * capacity + slot_rank
    placement_plan = (
        slot_index[:, None] == lax.broadcasted_iota(jnp.int32, (tile_count, slot_total), 1)
    ).astype(jnp.float32)
    payload = jnp.concatenate(
        [
            jnp.where(live_rows[:, None], records[0:5].transpose(1, 0, 2), 0.0),
            cell_ids.astype(jnp.float32)[:, None],
        ],
        1,
    )
    payload = jnp.concatenate([jnp.abs(payload[:, 0:1]), payload[:, 1:]], 1)
    outbound = jnp.einsum(
        "ts,tq->sq",
        placement_plan,
        payload.reshape(tile_count, 6 * row_count),
        precision=lax.Precision.HIGHEST,
    ).reshape(slot_total, 6, row_count)
    arrived = lax.all_to_all(outbound, ("stream", "cross"), split_axis=0, concat_axis=0, tiled=True)
    outbound, state_and_visc = lax.optimization_barrier(
        (outbound, jnp.concatenate([fluid_state, viscosity[None]], 0))
    )
    state_visc = face_halo(state_and_visc)
    state_pad = state_visc[0:5]
    visc_pad = state_visc[5]

    cells = jnp.round(arrived[:, 5]).astype(jnp.int32).reshape(faces)
    plane = cells // vertical_cells
    depth = cells % vertical_cells
    depth_hot = (
        depth[:, None] == lax.broadcasted_iota(jnp.int32, (faces, vertical_cells), 1)
    )
    plane_rows = plane[None, :] == lax.broadcasted_iota(jnp.int32, (plane_count, faces), 0)
    spread = jnp.where(
        plane_rows[None], arrived[:, 0:5].transpose(1, 0, 2).reshape(5, 1, faces), 0.0
    )
    source = jnp.einsum(
        "cpf,fd->cpd", spread, depth_hot.astype(jnp.float32), precision=lax.Precision.HIGHEST
    )
    source = source.reshape(5, cells_x, cells_y, vertical_cells)

    middle = shifted(state_pad, 1, 0, 0) + viscous(state_pad, visc_pad) + source
    middle_pad = face_halo(middle)
    new_state = middle + viscous(middle_pad, visc_pad)

    flat_state = new_state.reshape(5, plane_count, vertical_cells)
    kinetic = (
        flat_state[1] * flat_state[1]
        + flat_state[2] * flat_state[2]
        + flat_state[3] * flat_state[3]
    )
    pressure = 0.4 * (flat_state[4] - 0.5 * kinetic / flat_state[0])
    picked = exact_dot("fd,dp->fp", pressure.T, depth_hot.astype(jnp.bfloat16), False)
    plane_cols = plane[:, None] == lax.broadcasted_iota(jnp.int32, (faces, plane_count), 1)
    face_pressure = jnp.sum(jnp.where(plane_cols, picked, 0.0), axis=1)
    returned = lax.all_to_all(
        face_pressure.reshape(1, slot_total, row_count),
        ("stream", "cross"),
        split_axis=1,
        concat_axis=1,
        tiled=True,
    )
    home_pressure = jnp.einsum(
        "ts,sr->tr", placement_plan, returned[0], precision=lax.Precision.HIGHEST
    )
    face_loads = jnp.where(live_rows[None], records[5:8], 0.0) * home_pressure[None]
    return (new_state, face_loads)


def solution(mesh):
    placed = (
        P("stream", "cross", "gore"),
        P(None, "stream", "cross", "gore"),
        P("stream", "cross", "gore"),
        P(None, ("stream", "cross", "gore"), None),
        P(("stream", "cross", "gore"), None),
        P(("stream", "cross", "gore"), None),
        P(("stream", "cross", "gore")),
    )
    return jax.shard_map(
        shards,
        mesh=mesh,
        in_specs=placed,
        out_specs=(P(None, "stream", "cross", "gore"), P(None, ("stream", "cross", "gore"), None)),
        check_vma=False,
    )
```

```python
import jax
import jax.numpy as jnp
from jax import lax
from jax.sharding import PartitionSpec as P


SIDES = (("stream", 1), ("cross", 2), ("gore", 3))


def face_halo(block):
    wide = block
    for axis, dim in SIDES:
        count = lax.axis_size(axis)
        index = lax.axis_index(axis)
        odd = index % 2 == 1
        extent = block.shape[dim]
        last = lax.slice_in_dim(block, extent - 1, None, axis=dim)
        first = lax.slice_in_dim(block, 0, 1, axis=dim)
        pairs_a = [(i, i ^ 1) for i in range(count) if (i ^ 1) < count]
        pairs_b = [(i, j) for i in range(1, count) for j in (i - 1, i + 1) if j >= 1 and j < count and (min(i, j) % 2 == 1)]
        from_a = lax.ppermute(jnp.where(odd, first, last), axis, pairs_a)
        if pairs_b:
            from_b = lax.ppermute(jnp.where(odd, last, first), axis, pairs_b)
        else:
            from_b = jnp.zeros_like(from_a)
        low = jnp.where(odd, from_a, from_b)
        high = jnp.where(odd, from_b, from_a)
        widths = [(0, 0)] + [(1, 1) if d < dim else (0, 0) for d in range(1, 4)]
        wide = jnp.concatenate([jnp.pad(low, widths), wide, jnp.pad(high, widths)], axis=dim)
    return wide


def harmonic(first_visc, second_visc):
    summed = first_visc + second_visc
    denominator = jnp.where(summed > 0, summed, 1.0)
    return 2.0 * first_visc * second_visc / denominator


def shifted(values, leading, spatial, offset):
    value_portions = [slice(None)] * leading
    for position in range(3):
        extent = values.shape[leading + position]
        if position == spatial:
            value_portions.append(slice(1 + offset, extent - 1 + offset))
        else:
            value_portions.append(slice(1, extent - 1))
    return values[tuple(value_portions)]


def viscous(field, visc):
    centre = shifted(field, 1, 0, 0)
    centre_visc = shifted(visc, 0, 0, 0)
    change = jnp.zeros_like(centre)
    for spatial in range(3):
        for offset in (1, -1):
            face_visc = harmonic(centre_visc, shifted(visc, 0, spatial, offset))
            change = change + face_visc[None] * (shifted(field, 1, spatial, offset) - centre)
    return change


def split_high(values):
    scaled = values * jnp.float32(65537.0)
    high = scaled - (scaled - values)
    return (high, values - high)


def three_bf16(values):
    first, rest = split_high(values)
    second, third = split_high(rest)
    return tuple(part.astype(jnp.bfloat16) for part in (first, second, third))


def exact_dot(spec, values, onehot, values_first):
    stacked = jnp.stack(three_bf16(values), 0)
    left, right = spec.split("->")[0].split(",")
    output = spec.split("->")[1]
    if values_first:
        terms = jnp.einsum(
            "k" + left + "," + right + "->k" + output, stacked, onehot,
            preferred_element_type=jnp.float32,
        )
    else:
        terms = jnp.einsum(
            left + ",k" + right + "->k" + output, onehot, stacked,
            preferred_element_type=jnp.float32,
        )
    return terms[0] + terms[1] + terms[2]


def shards(density, momentum_energy, viscosity, records, cell_ids, routes, lengths):
    fluid_state = jnp.concatenate([density[None], momentum_energy], 0)
    cells_x, cells_y, vertical_cells = density.shape
    plane_count = cells_x * cells_y
    tile_count = records.shape[1]
    row_count = records.shape[2]
    blocks = lax.axis_size("stream") * lax.axis_size("cross")
    capacity = max(2, 2 * tile_count // blocks)
    slot_total = blocks * capacity
    faces = slot_total * row_count

    live_rows = lax.broadcasted_iota(jnp.int32, (tile_count, row_count), 1) < lengths[:, None]
    target = routes[:, 0]
    earlier = lax.broadcasted_iota(jnp.int32, (tile_count, tile_count), 1) < lax.broadcasted_iota(
        jnp.int32, (tile_count, tile_count), 0
    )
    slot_rank = jnp.sum(
        (earlier & (target[None, :] == target[:, None])).astype(jnp.int32), axis=1
    )
    slot_index = target * capacity + slot_rank
    placement_plan = (
        slot_index[:, None] == lax.broadcasted_iota(jnp.int32, (tile_count, slot_total), 1)
    ).astype(jnp.float32)
    live_cells = jnp.where(live_rows, cell_ids, -1).astype(jnp.float32)
    payload = jnp.concatenate(
        [records[0:5].transpose(1, 0, 2), live_cells[:, None]], 1
    )
    outbound = jnp.einsum(
        "ts,tq->sq",
        placement_plan,
        payload.reshape(tile_count, 6 * row_count),
        precision=lax.Precision.HIGHEST,
    ).reshape(slot_total, 6, row_count)
    arrived = lax.all_to_all(outbound, ("stream", "cross"), split_axis=0, concat_axis=0, tiled=True)
    outbound, state_and_visc = lax.optimization_barrier(
        (outbound, jnp.concatenate([fluid_state, viscosity[None]], 0))
    )
    state_visc = face_halo(state_and_visc)
    state_pad = state_visc[0:5]
    visc_pad = state_visc[5]

    cells = jnp.round(arrived[:, 5]).astype(jnp.int32).reshape(faces)
    plane = cells // vertical_cells
    depth = cells % vertical_cells
    depth_hot = (
        depth[:, None] == lax.broadcasted_iota(jnp.int32, (faces, vertical_cells), 1)
    )
    plane_rows = plane[None, :] == lax.broadcasted_iota(jnp.int32, (plane_count, faces), 0)
    arrived_values = arrived[:, 0:5].transpose(1, 0, 2).reshape(5, faces)
    arrived_values = jnp.concatenate([jnp.abs(arrived_values[0:1]), arrived_values[1:5]], 0)
    spread = jnp.where(plane_rows[None], arrived_values[:, None, :], 0.0)
    source = jnp.einsum(
        "cpf,fd->cpd", spread, depth_hot.astype(jnp.float32), precision=lax.Precision.HIGHEST
    )
    source = source.reshape(5, cells_x, cells_y, vertical_cells)

    middle = shifted(state_pad, 1, 0, 0) + viscous(state_pad, visc_pad) + source
    middle_pad = face_halo(middle)
    new_state = middle + viscous(middle_pad, visc_pad)

    flat_state = new_state.reshape(5, plane_count, vertical_cells)
    kinetic = (
        flat_state[1] * flat_state[1]
        + flat_state[2] * flat_state[2]
        + flat_state[3] * flat_state[3]
    )
    pressure = 0.4 * (flat_state[4] - 0.5 * kinetic / flat_state[0])
    picked = exact_dot("fd,dp->fp", pressure.T, depth_hot.astype(jnp.bfloat16), False)
    plane_cols = plane[:, None] == lax.broadcasted_iota(jnp.int32, (faces, plane_count), 1)
    face_pressure = jnp.sum(jnp.where(plane_cols, picked, 0.0), axis=1)
    returned = lax.all_to_all(
        face_pressure.reshape(1, slot_total, row_count),
        ("stream", "cross"),
        split_axis=1,
        concat_axis=1,
        tiled=True,
    )
    home_pressure = jnp.einsum(
        "ts,sr->tr", placement_plan, returned[0], precision=lax.Precision.HIGHEST
    )
    face_loads = jnp.where(live_rows[None], records[5:8], 0.0) * home_pressure[None]
    return (new_state, face_loads)


def solution(mesh):
    placed = (
        P("stream", "cross", "gore"),
        P(None, "stream", "cross", "gore"),
        P("stream", "cross", "gore"),
        P(None, ("stream", "cross", "gore"), None),
        P(("stream", "cross", "gore"), None),
        P(("stream", "cross", "gore"), None),
        P(("stream", "cross", "gore")),
    )
    return jax.shard_map(
        shards,
        mesh=mesh,
        in_specs=placed,
        out_specs=(P(None, "stream", "cross", "gore"), P(None, ("stream", "cross", "gore"), None)),
        check_vma=False,
    )
```

```python
import jax
import jax.numpy as jnp
from jax import lax
from jax.sharding import PartitionSpec as P


SIDES = (("stream", 1), ("cross", 2), ("gore", 3))


def face_halo(block):
    wide = block
    for axis, dim in SIDES:
        count = lax.axis_size(axis)
        index = lax.axis_index(axis)
        odd = index % 2 == 1
        extent = block.shape[dim]
        last = lax.slice_in_dim(block, extent - 1, None, axis=dim)
        first = lax.slice_in_dim(block, 0, 1, axis=dim)
        pairs_a = [(i, i ^ 1) for i in range(count) if (i ^ 1) < count]
        pairs_b = [(i, j) for i in range(1, count) for j in (i - 1, i + 1) if j >= 1 and j < count and (min(i, j) % 2 == 1)]
        from_a = lax.ppermute(jnp.where(odd, first, last), axis, pairs_a)
        if pairs_b:
            from_b = lax.ppermute(jnp.where(odd, last, first), axis, pairs_b)
        else:
            from_b = jnp.zeros_like(from_a)
        low = jnp.where(odd, from_a, from_b)
        high = jnp.where(odd, from_b, from_a)
        widths = [(0, 0)] + [(1, 1) if d < dim else (0, 0) for d in range(1, 4)]
        wide = jnp.concatenate([jnp.pad(low, widths), wide, jnp.pad(high, widths)], axis=dim)
    return wide


def harmonic(first_visc, second_visc):
    summed = first_visc + second_visc
    denominator = jnp.where(summed > 0, summed, 1.0)
    return 2.0 * first_visc * second_visc / denominator


def shifted(values, leading, spatial, offset):
    value_portions = [slice(None)] * leading
    for position in range(3):
        extent = values.shape[leading + position]
        if position == spatial:
            value_portions.append(slice(1 + offset, extent - 1 + offset))
        else:
            value_portions.append(slice(1, extent - 1))
    return values[tuple(value_portions)]


def viscous(field, visc):
    centre = shifted(field, 1, 0, 0)
    centre_visc = shifted(visc, 0, 0, 0)
    change = jnp.zeros_like(centre)
    for spatial in range(3):
        for offset in (1, -1):
            face_visc = harmonic(centre_visc, shifted(visc, 0, spatial, offset))
            change = change + face_visc[None] * (shifted(field, 1, spatial, offset) - centre)
    return change


def split_high(values):
    scaled = values * jnp.float32(65537.0)
    high = scaled - (scaled - values)
    return (high, values - high)


def three_bf16(values):
    first, rest = split_high(values)
    second, third = split_high(rest)
    return tuple(part.astype(jnp.bfloat16) for part in (first, second, third))


def exact_dot(spec, values, onehot, values_first):
    stacked = jnp.stack(three_bf16(values), 0)
    left, right = spec.split("->")[0].split(",")
    output = spec.split("->")[1]
    if values_first:
        terms = jnp.einsum(
            "k" + left + "," + right + "->k" + output, stacked, onehot,
            preferred_element_type=jnp.float32,
        )
    else:
        terms = jnp.einsum(
            left + ",k" + right + "->k" + output, onehot, stacked,
            preferred_element_type=jnp.float32,
        )
    return terms[0] + terms[1] + terms[2]


def shards(density, momentum_energy, viscosity, records, cell_ids, routes, lengths):
    fluid_state = jnp.concatenate([density[None], momentum_energy], 0)
    cells_x, cells_y, vertical_cells = density.shape
    plane_count = cells_x * cells_y
    tile_count = records.shape[1]
    row_count = records.shape[2]
    blocks = lax.axis_size("stream") * lax.axis_size("cross")
    capacity = max(2, 2 * tile_count // blocks)
    slot_total = blocks * capacity
    faces = slot_total * row_count

    live_rows = lax.broadcasted_iota(jnp.int32, (tile_count, row_count), 1) < lengths[:, None]
    target = routes[:, 0]
    earlier = lax.broadcasted_iota(jnp.int32, (tile_count, tile_count), 1) < lax.broadcasted_iota(
        jnp.int32, (tile_count, tile_count), 0
    )
    slot_rank = jnp.sum(
        (earlier & (target[None, :] == target[:, None])).astype(jnp.int32), axis=1
    )
    slot_index = target * capacity + slot_rank
    placement_plan = (
        slot_index[:, None] == lax.broadcasted_iota(jnp.int32, (tile_count, slot_total), 1)
    ).astype(jnp.float32)
    live_cells = jnp.where(live_rows, cell_ids, -1).astype(jnp.float32)
    payload = jnp.concatenate([records[0:5], live_cells[None]], 0)
    outbound = jnp.einsum(
        "ts,ctr->csr", placement_plan, payload, precision=lax.Precision.HIGHEST
    )
    arrived = lax.all_to_all(outbound, ("stream", "cross"), split_axis=1, concat_axis=1, tiled=True)
    outbound, state_and_visc, load_rows = lax.optimization_barrier(
        (
            outbound,
            jnp.concatenate([fluid_state, viscosity[None]], 0),
            jnp.where(live_rows[None], records[5:8], 0.0),
        )
    )
    state_visc = face_halo(state_and_visc)
    state_pad = state_visc[0:5]
    visc_pad = state_visc[5]

    cells = jnp.round(arrived[5]).astype(jnp.int32).reshape(faces)
    plane = cells // vertical_cells
    depth = cells % vertical_cells
    depth_hot = (
        depth[:, None] == lax.broadcasted_iota(jnp.int32, (faces, vertical_cells), 1)
    )
    plane_rows = plane[None, :] == lax.broadcasted_iota(jnp.int32, (plane_count, faces), 0)
    arrived_values = arrived[0:5].reshape(5, faces)
    arrived_values = jnp.concatenate([jnp.abs(arrived_values[0:1]), arrived_values[1:5]], 0)
    spread = jnp.where(plane_rows[None], arrived_values[:, None, :], 0.0)
    source = jnp.einsum(
        "cpf,fd->cpd", spread, depth_hot.astype(jnp.float32), precision=lax.Precision.HIGHEST
    )
    source = source.reshape(5, cells_x, cells_y, vertical_cells)

    middle = shifted(state_pad, 1, 0, 0) + viscous(state_pad, visc_pad) + source
    middle_pad = face_halo(middle)
    new_state = middle + viscous(middle_pad, visc_pad)

    flat_state = new_state.reshape(5, plane_count, vertical_cells)
    kinetic = (
        flat_state[1] * flat_state[1]
        + flat_state[2] * flat_state[2]
        + flat_state[3] * flat_state[3]
    )
    pressure = 0.4 * (flat_state[4] - 0.5 * kinetic / flat_state[0])
    picked = exact_dot("fd,dp->fp", pressure.T, depth_hot.astype(jnp.bfloat16), False)
    plane_cols = plane[:, None] == lax.broadcasted_iota(jnp.int32, (faces, plane_count), 1)
    face_pressure = jnp.sum(jnp.where(plane_cols, picked, 0.0), axis=1)
    returned = lax.all_to_all(
        face_pressure.reshape(1, slot_total, row_count),
        ("stream", "cross"),
        split_axis=1,
        concat_axis=1,
        tiled=True,
    )
    home_pressure = jnp.einsum(
        "ts,sr->tr", placement_plan, returned[0], precision=lax.Precision.HIGHEST
    )
    face_loads = load_rows * home_pressure[None]
    return (new_state, face_loads)


def solution(mesh):
    placed = (
        P("stream", "cross", "gore"),
        P(None, "stream", "cross", "gore"),
        P("stream", "cross", "gore"),
        P(None, ("stream", "cross", "gore"), None),
        P(("stream", "cross", "gore"), None),
        P(("stream", "cross", "gore"), None),
        P(("stream", "cross", "gore")),
    )
    return jax.shard_map(
        shards,
        mesh=mesh,
        in_specs=placed,
        out_specs=(P(None, "stream", "cross", "gore"), P(None, ("stream", "cross", "gore"), None)),
        check_vma=False,
    )
```

```python
import jax
import jax.numpy as jnp
from jax import lax
from jax.sharding import PartitionSpec as P


SIDES = (("stream", 1), ("cross", 2), ("gore", 3))


def face_halo(block):
    wide = block
    for axis, dim in SIDES:
        count = lax.axis_size(axis)
        index = lax.axis_index(axis)
        odd = index % 2 == 1
        extent = block.shape[dim]
        last = lax.slice_in_dim(block, extent - 1, None, axis=dim)
        first = lax.slice_in_dim(block, 0, 1, axis=dim)
        pairs_a = [(i, i ^ 1) for i in range(count) if (i ^ 1) < count]
        pairs_b = [(i, j) for i in range(1, count) for j in (i - 1, i + 1) if j >= 1 and j < count and (min(i, j) % 2 == 1)]
        from_a = lax.ppermute(jnp.where(odd, first, last), axis, pairs_a)
        if pairs_b:
            from_b = lax.ppermute(jnp.where(odd, last, first), axis, pairs_b)
        else:
            from_b = jnp.zeros_like(from_a)
        low = jnp.where(odd, from_a, from_b)
        high = jnp.where(odd, from_b, from_a)
        widths = [(0, 0)] + [(1, 1) if d < dim else (0, 0) for d in range(1, 4)]
        wide = jnp.concatenate([jnp.pad(low, widths), wide, jnp.pad(high, widths)], axis=dim)
    return wide


def harmonic(first_visc, second_visc):
    summed = first_visc + second_visc
    denominator = jnp.where(summed > 0, summed, 1.0)
    return 2.0 * first_visc * second_visc / denominator


def shifted(values, leading, spatial, offset):
    value_portions = [slice(None)] * leading
    for position in range(3):
        extent = values.shape[leading + position]
        if position == spatial:
            value_portions.append(slice(1 + offset, extent - 1 + offset))
        else:
            value_portions.append(slice(1, extent - 1))
    return values[tuple(value_portions)]


def viscous(field, visc):
    centre = shifted(field, 1, 0, 0)
    centre_visc = shifted(visc, 0, 0, 0)
    change = jnp.zeros_like(centre)
    for spatial in range(3):
        for offset in (1, -1):
            face_visc = harmonic(centre_visc, shifted(visc, 0, spatial, offset))
            change = change + face_visc[None] * (shifted(field, 1, spatial, offset) - centre)
    return change


def split_high(values):
    scaled = values * jnp.float32(65537.0)
    high = scaled - (scaled - values)
    return (high, values - high)


def three_bf16(values):
    first, rest = split_high(values)
    second, third = split_high(rest)
    return tuple(part.astype(jnp.bfloat16) for part in (first, second, third))


def exact_dot(spec, values, onehot, values_first):
    stacked = jnp.stack(three_bf16(values), 0)
    left, right = spec.split("->")[0].split(",")
    output = spec.split("->")[1]
    if values_first:
        terms = jnp.einsum(
            "k" + left + "," + right + "->k" + output, stacked, onehot,
            preferred_element_type=jnp.float32,
        )
    else:
        terms = jnp.einsum(
            left + ",k" + right + "->k" + output, onehot, stacked,
            preferred_element_type=jnp.float32,
        )
    return terms[0] + terms[1] + terms[2]


def shards(density, momentum_energy, viscosity, records, cell_ids, routes, lengths):
    fluid_state = jnp.concatenate([density[None], momentum_energy], 0)
    cells_x, cells_y, vertical_cells = density.shape
    plane_count = cells_x * cells_y
    tile_count = records.shape[1]
    row_count = records.shape[2]
    blocks = lax.axis_size("stream") * lax.axis_size("cross")
    capacity = max(2, 2 * tile_count // blocks)
    slot_total = blocks * capacity
    faces = slot_total * row_count

    live_rows = lax.broadcasted_iota(jnp.int32, (tile_count, row_count), 1) < lengths[:, None]
    target = routes[:, 0]
    earlier = lax.broadcasted_iota(jnp.int32, (tile_count, tile_count), 1) < lax.broadcasted_iota(
        jnp.int32, (tile_count, tile_count), 0
    )
    slot_rank = jnp.sum(
        (earlier & (target[None, :] == target[:, None])).astype(jnp.int32), axis=1
    )
    slot_index = target * capacity + slot_rank
    placement_plan = (
        slot_index[:, None] == lax.broadcasted_iota(jnp.int32, (tile_count, slot_total), 1)
    ).astype(jnp.float32)
    live_cells = jnp.where(live_rows, cell_ids, -1).astype(jnp.float32)
    payload = jnp.concatenate([records[0:5], live_cells[None]], 0)
    outbound = jnp.einsum(
        "ts,ctr->csr", placement_plan, payload, precision=lax.Precision.HIGHEST
    )
    arrived = lax.all_to_all(outbound, ("stream", "cross"), split_axis=1, concat_axis=1, tiled=True)
    outbound, state_and_visc = lax.optimization_barrier(
        (outbound, jnp.concatenate([fluid_state, viscosity[None]], 0))
    )
    state_visc = face_halo(state_and_visc)
    state_pad = state_visc[0:5]
    visc_pad = state_visc[5]

    cells = jnp.round(arrived[5]).astype(jnp.int32).reshape(faces)
    plane = cells // vertical_cells
    depth = cells % vertical_cells
    depth_hot = (
        depth[:, None] == lax.broadcasted_iota(jnp.int32, (faces, vertical_cells), 1)
    )
    plane_rows = plane[None, :] == lax.broadcasted_iota(jnp.int32, (plane_count, faces), 0)
    arrived_values = arrived[0:5].reshape(5, faces)
    arrived_values = jnp.concatenate([jnp.abs(arrived_values[0:1]), arrived_values[1:5]], 0)
    spread = jnp.where(plane_rows[None], arrived_values[:, None, :], 0.0)
    source = jnp.einsum(
        "cpf,fd->cpd", spread, depth_hot.astype(jnp.float32), precision=lax.Precision.HIGH
    )
    source = source.reshape(5, cells_x, cells_y, vertical_cells)

    middle = shifted(state_pad, 1, 0, 0) + viscous(state_pad, visc_pad) + source
    middle_pad = face_halo(middle)
    new_state = middle + viscous(middle_pad, visc_pad)

    flat_state = new_state.reshape(5, plane_count, vertical_cells)
    kinetic = (
        flat_state[1] * flat_state[1]
        + flat_state[2] * flat_state[2]
        + flat_state[3] * flat_state[3]
    )
    pressure = 0.4 * (flat_state[4] - 0.5 * kinetic / flat_state[0])
    picked = exact_dot("fd,dp->fp", pressure.T, depth_hot.astype(jnp.bfloat16), False)
    plane_cols = plane[:, None] == lax.broadcasted_iota(jnp.int32, (faces, plane_count), 1)
    face_pressure = jnp.sum(jnp.where(plane_cols, picked, 0.0), axis=1)
    returned = lax.all_to_all(
        face_pressure.reshape(1, slot_total, row_count),
        ("stream", "cross"),
        split_axis=1,
        concat_axis=1,
        tiled=True,
    )
    home_pressure = jnp.einsum(
        "ts,sr->tr", placement_plan, returned[0], precision=lax.Precision.HIGHEST
    )
    face_loads = jnp.where(live_rows[None], records[5:8], 0.0) * home_pressure[None]
    return (new_state, face_loads)


def solution(mesh):
    placed = (
        P("stream", "cross", "gore"),
        P(None, "stream", "cross", "gore"),
        P("stream", "cross", "gore"),
        P(None, ("stream", "cross", "gore"), None),
        P(("stream", "cross", "gore"), None),
        P(("stream", "cross", "gore"), None),
        P(("stream", "cross", "gore")),
    )
    return jax.shard_map(
        shards,
        mesh=mesh,
        in_specs=placed,
        out_specs=(P(None, "stream", "cross", "gore"), P(None, ("stream", "cross", "gore"), None)),
        check_vma=False,
    )
```

```python
import jax
import jax.numpy as jnp
from jax import lax
from jax.experimental import pallas as pl
from jax.sharding import PartitionSpec as P


SIDES = (("stream", 1), ("cross", 2), ("gore", 3))


def face_halo(block):
    wide = block
    for axis, dim in SIDES:
        count = lax.axis_size(axis)
        index = lax.axis_index(axis)
        odd = index % 2 == 1
        extent = block.shape[dim]
        last = lax.slice_in_dim(block, extent - 1, None, axis=dim)
        first = lax.slice_in_dim(block, 0, 1, axis=dim)
        pairs_a = [(i, i ^ 1) for i in range(count) if (i ^ 1) < count]
        pairs_b = [(i, j) for i in range(1, count) for j in (i - 1, i + 1) if j >= 1 and j < count and (min(i, j) % 2 == 1)]
        from_a = lax.ppermute(jnp.where(odd, first, last), axis, pairs_a)
        if pairs_b:
            from_b = lax.ppermute(jnp.where(odd, last, first), axis, pairs_b)
        else:
            from_b = jnp.zeros_like(from_a)
        low = jnp.where(odd, from_a, from_b)
        high = jnp.where(odd, from_b, from_a)
        widths = [(0, 0)] + [(1, 1) if d < dim else (0, 0) for d in range(1, 4)]
        wide = jnp.concatenate([jnp.pad(low, widths), wide, jnp.pad(high, widths)], axis=dim)
    return wide


def harmonic(first_visc, second_visc):
    summed = first_visc + second_visc
    denominator = jnp.where(summed > 0, summed, 1.0)
    return 2.0 * first_visc * second_visc / denominator


def shifted(values, leading, spatial, offset):
    value_portions = [slice(None)] * leading
    for position in range(3):
        extent = values.shape[leading + position]
        if position == spatial:
            value_portions.append(slice(1 + offset, extent - 1 + offset))
        else:
            value_portions.append(slice(1, extent - 1))
    return values[tuple(value_portions)]


def viscous(field, visc):
    centre = shifted(field, 1, 0, 0)
    centre_visc = shifted(visc, 0, 0, 0)
    change = jnp.zeros_like(centre)
    for spatial in range(3):
        for offset in (1, -1):
            face_visc = harmonic(centre_visc, shifted(visc, 0, spatial, offset))
            change = change + face_visc[None] * (shifted(field, 1, spatial, offset) - centre)
    return change


def split_high(values):
    scaled = values * jnp.float32(65537.0)
    high = scaled - (scaled - values)
    return (high, values - high)


def three_bf16(values):
    first, rest = split_high(values)
    second, third = split_high(rest)
    return tuple(part.astype(jnp.bfloat16) for part in (first, second, third))


def exact_dot(spec, values, onehot, values_first):
    stacked = jnp.stack(three_bf16(values), 0)
    left, right = spec.split("->")[0].split(",")
    output = spec.split("->")[1]
    if values_first:
        terms = jnp.einsum(
            "k" + left + "," + right + "->k" + output, stacked, onehot,
            preferred_element_type=jnp.float32,
        )
    else:
        terms = jnp.einsum(
            left + ",k" + right + "->k" + output, onehot, stacked,
            preferred_element_type=jnp.float32,
        )
    return terms[0] + terms[1] + terms[2]


def make_pack(tile_count, row_count, blocks, capacity):
    slot_total = blocks * capacity

    def pack_kernel(route_ref, length_ref, cell_ref, record_ref, out_ref):
        target = route_ref[...]
        tile_iota_row = lax.broadcasted_iota(jnp.int32, (tile_count, tile_count), 1)
        tile_iota_col = lax.broadcasted_iota(jnp.int32, (tile_count, tile_count), 0)
        lengths_col = jnp.sum(
            jnp.where(tile_iota_row == tile_iota_col, length_ref[...], 0), axis=1, keepdims=True
        )
        block_hot = (
            target == lax.broadcasted_iota(jnp.int32, (tile_count, blocks), 1)
        ).astype(jnp.float32)
        same = lax.dot_general(
            block_hot, block_hot, (((1,), (1,)), ((), ())), preferred_element_type=jnp.float32
        )
        rank = jnp.sum(jnp.where(tile_iota_row < tile_iota_col, same, 0.0), axis=1, keepdims=True)
        slot = target * capacity + rank.astype(jnp.int32)
        slot_hot = (
            slot == lax.broadcasted_iota(jnp.int32, (tile_count, slot_total), 1)
        ).astype(jnp.float32)
        eye = (
            lax.broadcasted_iota(jnp.int32, (slot_total, slot_total), 0)
            == lax.broadcasted_iota(jnp.int32, (slot_total, slot_total), 1)
        ).astype(jnp.float32)
        plan = lax.dot_general(
            eye, slot_hot, (((1,), (1,)), ((), ())), preferred_element_type=jnp.float32
        )
        live = lax.broadcasted_iota(jnp.int32, (tile_count, row_count), 1) < lengths_col
        for comp in range(6):
            if comp < 5:
                rows = record_ref[comp]
            else:
                rows = jnp.where(live, cell_ref[...], -1).astype(jnp.float32)
            out_ref[:, comp * row_count:(comp + 1) * row_count] = jnp.dot(
                plan, rows, precision=lax.Precision.HIGHEST, preferred_element_type=jnp.float32
            )

    def pack(routes, lengths, cell_ids, records):
        return pl.pallas_call(
            pack_kernel,
            out_shape=jax.ShapeDtypeStruct((slot_total, 6 * row_count), jnp.float32),
        )(routes, lengths.reshape(1, tile_count), cell_ids, records)
    return pack


def shards(density, momentum_energy, viscosity, records, cell_ids, routes, lengths):
    fluid_state = jnp.concatenate([density[None], momentum_energy], 0)
    cells_x, cells_y, vertical_cells = density.shape
    plane_count = cells_x * cells_y
    tile_count = records.shape[1]
    row_count = records.shape[2]
    blocks = lax.axis_size("stream") * lax.axis_size("cross")
    capacity = max(2, 2 * tile_count // blocks)
    slot_total = blocks * capacity
    faces = slot_total * row_count

    live_rows = lax.broadcasted_iota(jnp.int32, (tile_count, row_count), 1) < lengths[:, None]
    target = routes[:, 0]
    earlier = lax.broadcasted_iota(jnp.int32, (tile_count, tile_count), 1) < lax.broadcasted_iota(
        jnp.int32, (tile_count, tile_count), 0
    )
    slot_rank = jnp.sum(
        (earlier & (target[None, :] == target[:, None])).astype(jnp.int32), axis=1
    )
    slot_index = target * capacity + slot_rank
    placement_plan = (
        slot_index[:, None] == lax.broadcasted_iota(jnp.int32, (tile_count, slot_total), 1)
    ).astype(jnp.float32)
    pack = make_pack(tile_count, row_count, blocks, capacity)
    outbound = pack(routes, lengths, cell_ids, records)
    arrived = lax.all_to_all(outbound, ("stream", "cross"), split_axis=0, concat_axis=0, tiled=True)
    outbound, state_and_visc = lax.optimization_barrier(
        (outbound, jnp.concatenate([fluid_state, viscosity[None]], 0))
    )
    state_visc = face_halo(state_and_visc)
    state_pad = state_visc[0:5]
    visc_pad = state_visc[5]

    cells = jnp.round(arrived[:, 5 * row_count:]).astype(jnp.int32).reshape(faces)
    plane = cells // vertical_cells
    depth = cells % vertical_cells
    depth_hot = (
        depth[:, None] == lax.broadcasted_iota(jnp.int32, (faces, vertical_cells), 1)
    )
    plane_rows = plane[None, :] == lax.broadcasted_iota(jnp.int32, (plane_count, faces), 0)
    arrived_values = jnp.stack(
        [arrived[:, c * row_count:(c + 1) * row_count].reshape(faces) for c in range(5)], 0
    )
    arrived_values = jnp.concatenate([jnp.abs(arrived_values[0:1]), arrived_values[1:5]], 0)
    spread = jnp.where(plane_rows[None], arrived_values[:, None, :], 0.0)
    source = jnp.einsum(
        "cpf,fd->cpd", spread, depth_hot.astype(jnp.float32), precision=lax.Precision.HIGH
    )
    source = source.reshape(5, cells_x, cells_y, vertical_cells)

    middle = shifted(state_pad, 1, 0, 0) + viscous(state_pad, visc_pad) + source
    middle_pad = face_halo(middle)
    new_state = middle + viscous(middle_pad, visc_pad)

    flat_state = new_state.reshape(5, plane_count, vertical_cells)
    kinetic = (
        flat_state[1] * flat_state[1]
        + flat_state[2] * flat_state[2]
        + flat_state[3] * flat_state[3]
    )
    pressure = 0.4 * (flat_state[4] - 0.5 * kinetic / flat_state[0])
    picked = exact_dot("fd,dp->fp", pressure.T, depth_hot.astype(jnp.bfloat16), False)
    plane_cols = plane[:, None] == lax.broadcasted_iota(jnp.int32, (faces, plane_count), 1)
    face_pressure = jnp.sum(jnp.where(plane_cols, picked, 0.0), axis=1)
    returned = lax.all_to_all(
        face_pressure.reshape(1, slot_total, row_count),
        ("stream", "cross"),
        split_axis=1,
        concat_axis=1,
        tiled=True,
    )
    home_pressure = jnp.einsum(
        "ts,sr->tr", placement_plan, returned[0], precision=lax.Precision.HIGHEST
    )
    face_loads = jnp.where(live_rows[None], records[5:8], 0.0) * home_pressure[None]
    return (new_state, face_loads)


def solution(mesh):
    placed = (
        P("stream", "cross", "gore"),
        P(None, "stream", "cross", "gore"),
        P("stream", "cross", "gore"),
        P(None, ("stream", "cross", "gore"), None),
        P(("stream", "cross", "gore"), None),
        P(("stream", "cross", "gore"), None),
        P(("stream", "cross", "gore")),
    )
    return jax.shard_map(
        shards,
        mesh=mesh,
        in_specs=placed,
        out_specs=(P(None, "stream", "cross", "gore"), P(None, ("stream", "cross", "gore"), None)),
        check_vma=False,
    )
```

```python
import jax
import jax.numpy as jnp
from jax import lax
from jax.experimental import pallas as pl
from jax.sharding import PartitionSpec as P


SIDES = (("stream", 1), ("cross", 2), ("gore", 3))


def face_halo(block):
    wide = block
    for axis, dim in SIDES:
        count = lax.axis_size(axis)
        index = lax.axis_index(axis)
        odd = index % 2 == 1
        extent = block.shape[dim]
        last = lax.slice_in_dim(block, extent - 1, None, axis=dim)
        first = lax.slice_in_dim(block, 0, 1, axis=dim)
        pairs_a = [(i, i ^ 1) for i in range(count) if (i ^ 1) < count]
        pairs_b = [(i, j) for i in range(1, count) for j in (i - 1, i + 1) if j >= 1 and j < count and (min(i, j) % 2 == 1)]
        from_a = lax.ppermute(jnp.where(odd, first, last), axis, pairs_a)
        if pairs_b:
            from_b = lax.ppermute(jnp.where(odd, last, first), axis, pairs_b)
        else:
            from_b = jnp.zeros_like(from_a)
        low = jnp.where(odd, from_a, from_b)
        high = jnp.where(odd, from_b, from_a)
        widths = [(0, 0)] + [(1, 1) if d < dim else (0, 0) for d in range(1, 4)]
        wide = jnp.concatenate([jnp.pad(low, widths), wide, jnp.pad(high, widths)], axis=dim)
    return wide


def harmonic(first_visc, second_visc):
    summed = first_visc + second_visc
    denominator = jnp.where(summed > 0, summed, 1.0)
    return 2.0 * first_visc * second_visc / denominator


def shifted(values, leading, spatial, offset):
    value_portions = [slice(None)] * leading
    for position in range(3):
        extent = values.shape[leading + position]
        if position == spatial:
            value_portions.append(slice(1 + offset, extent - 1 + offset))
        else:
            value_portions.append(slice(1, extent - 1))
    return values[tuple(value_portions)]


def viscous(field, visc):
    centre = shifted(field, 1, 0, 0)
    centre_visc = shifted(visc, 0, 0, 0)
    change = jnp.zeros_like(centre)
    for spatial in range(3):
        for offset in (1, -1):
            face_visc = harmonic(centre_visc, shifted(visc, 0, spatial, offset))
            change = change + face_visc[None] * (shifted(field, 1, spatial, offset) - centre)
    return change


def split_high(values):
    scaled = values * jnp.float32(65537.0)
    high = scaled - (scaled - values)
    return (high, values - high)


def three_bf16(values):
    first, rest = split_high(values)
    second, third = split_high(rest)
    return tuple(part.astype(jnp.bfloat16) for part in (first, second, third))


def exact_dot(spec, values, onehot, values_first):
    stacked = jnp.stack(three_bf16(values), 0)
    left, right = spec.split("->")[0].split(",")
    output = spec.split("->")[1]
    if values_first:
        terms = jnp.einsum(
            "k" + left + "," + right + "->k" + output, stacked, onehot,
            preferred_element_type=jnp.float32,
        )
    else:
        terms = jnp.einsum(
            left + ",k" + right + "->k" + output, onehot, stacked,
            preferred_element_type=jnp.float32,
        )
    return terms[0] + terms[1] + terms[2]


def make_pack(tile_count, row_count, blocks, capacity):
    slot_total = blocks * capacity

    def pack_kernel(route_ref, length_ref, cell_ref, record_ref, out_ref, load_ref):
        tile_iota_row = lax.broadcasted_iota(jnp.int32, (tile_count, tile_count), 1)
        tile_iota_col = lax.broadcasted_iota(jnp.int32, (tile_count, tile_count), 0)
        diagonal = tile_iota_row == tile_iota_col
        target = jnp.sum(jnp.where(diagonal, route_ref[...], 0), axis=1, keepdims=True)
        lengths_col = jnp.sum(jnp.where(diagonal, length_ref[...], 0), axis=1, keepdims=True)
        block_hot = (
            target == lax.broadcasted_iota(jnp.int32, (tile_count, blocks), 1)
        ).astype(jnp.float32)
        same = lax.dot_general(
            block_hot, block_hot, (((1,), (1,)), ((), ())), preferred_element_type=jnp.float32
        )
        rank = jnp.sum(jnp.where(tile_iota_row < tile_iota_col, same, 0.0), axis=1, keepdims=True)
        slot = target * capacity + rank.astype(jnp.int32)
        slot_hot = (
            slot == lax.broadcasted_iota(jnp.int32, (tile_count, slot_total), 1)
        ).astype(jnp.float32)
        eye = (
            lax.broadcasted_iota(jnp.int32, (slot_total, slot_total), 0)
            == lax.broadcasted_iota(jnp.int32, (slot_total, slot_total), 1)
        ).astype(jnp.float32)
        plan = lax.dot_general(
            eye, slot_hot, (((1,), (1,)), ((), ())), preferred_element_type=jnp.float32
        )
        live = lax.broadcasted_iota(jnp.int32, (tile_count, row_count), 1) < lengths_col
        for comp in range(3):
            load_ref[comp] = jnp.where(live, record_ref[5 + comp], 0.0)
        for comp in range(6):
            if comp < 5:
                rows = record_ref[comp]
            else:
                rows = jnp.where(live, cell_ref[...], -1).astype(jnp.float32)
            out_ref[:, comp * row_count:(comp + 1) * row_count] = jnp.dot(
                plan, rows, precision=lax.Precision.HIGHEST, preferred_element_type=jnp.float32
            )

    def pack(routes, lengths, cell_ids, records):
        return pl.pallas_call(
            pack_kernel,
            out_shape=(
                jax.ShapeDtypeStruct((slot_total, 6 * row_count), jnp.float32),
                jax.ShapeDtypeStruct((3, tile_count, row_count), jnp.float32),
            ),
        )(routes.reshape(1, tile_count), lengths.reshape(1, tile_count), cell_ids, records)
    return pack


def shards(density, momentum_energy, viscosity, records, cell_ids, routes, lengths):
    fluid_state = jnp.concatenate([density[None], momentum_energy], 0)
    cells_x, cells_y, vertical_cells = density.shape
    plane_count = cells_x * cells_y
    tile_count = records.shape[1]
    row_count = records.shape[2]
    blocks = lax.axis_size("stream") * lax.axis_size("cross")
    capacity = max(2, 2 * tile_count // blocks)
    slot_total = blocks * capacity
    faces = slot_total * row_count

    target = routes[:, 0]
    earlier = lax.broadcasted_iota(jnp.int32, (tile_count, tile_count), 1) < lax.broadcasted_iota(
        jnp.int32, (tile_count, tile_count), 0
    )
    slot_rank = jnp.sum(
        (earlier & (target[None, :] == target[:, None])).astype(jnp.int32), axis=1
    )
    slot_index = target * capacity + slot_rank
    placement_plan = (
        slot_index[:, None] == lax.broadcasted_iota(jnp.int32, (tile_count, slot_total), 1)
    ).astype(jnp.float32)
    pack = make_pack(tile_count, row_count, blocks, capacity)
    outbound, load_rows = pack(routes, lengths, cell_ids, records)
    arrived = lax.all_to_all(outbound, ("stream", "cross"), split_axis=0, concat_axis=0, tiled=True)
    outbound, state_and_visc = lax.optimization_barrier(
        (outbound, jnp.concatenate([fluid_state, viscosity[None]], 0))
    )
    state_visc = face_halo(state_and_visc)
    state_pad = state_visc[0:5]
    visc_pad = state_visc[5]

    cells = jnp.round(arrived[:, 5 * row_count:]).astype(jnp.int32).reshape(faces)
    plane = cells // vertical_cells
    depth = cells % vertical_cells
    depth_hot = (
        depth[:, None] == lax.broadcasted_iota(jnp.int32, (faces, vertical_cells), 1)
    )
    plane_rows = plane[None, :] == lax.broadcasted_iota(jnp.int32, (plane_count, faces), 0)
    arrived_values = jnp.stack(
        [arrived[:, c * row_count:(c + 1) * row_count].reshape(faces) for c in range(5)], 0
    )
    arrived_values = jnp.concatenate([jnp.abs(arrived_values[0:1]), arrived_values[1:5]], 0)
    spread = jnp.where(plane_rows[None], arrived_values[:, None, :], 0.0)
    source = jnp.einsum(
        "cpf,fd->cpd", spread, depth_hot.astype(jnp.float32), precision=lax.Precision.HIGH
    )
    source = source.reshape(5, cells_x, cells_y, vertical_cells)

    middle = shifted(state_pad, 1, 0, 0) + viscous(state_pad, visc_pad) + source
    middle_pad = face_halo(middle)
    new_state = middle + viscous(middle_pad, visc_pad)

    flat_state = new_state.reshape(5, plane_count, vertical_cells)
    kinetic = (
        flat_state[1] * flat_state[1]
        + flat_state[2] * flat_state[2]
        + flat_state[3] * flat_state[3]
    )
    pressure = 0.4 * (flat_state[4] - 0.5 * kinetic / flat_state[0])
    picked = exact_dot("fd,dp->fp", pressure.T, depth_hot.astype(jnp.bfloat16), False)
    plane_cols = plane[:, None] == lax.broadcasted_iota(jnp.int32, (faces, plane_count), 1)
    face_pressure = jnp.sum(jnp.where(plane_cols, picked, 0.0), axis=1)
    returned = lax.all_to_all(
        face_pressure.reshape(1, slot_total, row_count),
        ("stream", "cross"),
        split_axis=1,
        concat_axis=1,
        tiled=True,
    )
    home_pressure = jnp.einsum(
        "ts,sr->tr", placement_plan, returned[0], precision=lax.Precision.HIGHEST
    )
    face_loads = load_rows * home_pressure[None]
    return (new_state, face_loads)


def solution(mesh):
    placed = (
        P("stream", "cross", "gore"),
        P(None, "stream", "cross", "gore"),
        P("stream", "cross", "gore"),
        P(None, ("stream", "cross", "gore"), None),
        P(("stream", "cross", "gore"), None),
        P(("stream", "cross", "gore"), None),
        P(("stream", "cross", "gore")),
    )
    return jax.shard_map(
        shards,
        mesh=mesh,
        in_specs=placed,
        out_specs=(P(None, "stream", "cross", "gore"), P(None, ("stream", "cross", "gore"), None)),
        check_vma=False,
    )
```

```python
import jax
import jax.numpy as jnp
from jax import lax
from jax.experimental import pallas as pl
from jax.sharding import PartitionSpec as P


SIDES = (("stream", 1), ("cross", 2), ("gore", 3))


def face_halo(block):
    wide = block
    for axis, dim in SIDES:
        count = lax.axis_size(axis)
        index = lax.axis_index(axis)
        odd = index % 2 == 1
        extent = block.shape[dim]
        last = lax.slice_in_dim(block, extent - 1, None, axis=dim)
        first = lax.slice_in_dim(block, 0, 1, axis=dim)
        pairs_a = [(i, i ^ 1) for i in range(count) if (i ^ 1) < count]
        pairs_b = [(i, j) for i in range(1, count) for j in (i - 1, i + 1) if j >= 1 and j < count and (min(i, j) % 2 == 1)]
        from_a = lax.ppermute(jnp.where(odd, first, last), axis, pairs_a)
        if pairs_b:
            from_b = lax.ppermute(jnp.where(odd, last, first), axis, pairs_b)
        else:
            from_b = jnp.zeros_like(from_a)
        low = jnp.where(odd, from_a, from_b)
        high = jnp.where(odd, from_b, from_a)
        widths = [(0, 0)] + [(1, 1) if d < dim else (0, 0) for d in range(1, 4)]
        wide = jnp.concatenate([jnp.pad(low, widths), wide, jnp.pad(high, widths)], axis=dim)
    return wide


def harmonic(first_visc, second_visc):
    summed = first_visc + second_visc
    denominator = jnp.where(summed > 0, summed, 1.0)
    return 2.0 * first_visc * second_visc / denominator


def shifted(values, leading, spatial, offset):
    value_portions = [slice(None)] * leading
    for position in range(3):
        extent = values.shape[leading + position]
        if position == spatial:
            value_portions.append(slice(1 + offset, extent - 1 + offset))
        else:
            value_portions.append(slice(1, extent - 1))
    return values[tuple(value_portions)]


def viscous(field, visc):
    centre = shifted(field, 1, 0, 0)
    centre_visc = shifted(visc, 0, 0, 0)
    change = jnp.zeros_like(centre)
    for spatial in range(3):
        for offset in (1, -1):
            face_visc = harmonic(centre_visc, shifted(visc, 0, spatial, offset))
            change = change + face_visc[None] * (shifted(field, 1, spatial, offset) - centre)
    return change


def split_high(values):
    scaled = values * jnp.float32(65537.0)
    high = scaled - (scaled - values)
    return (high, values - high)


def three_bf16(values):
    first, rest = split_high(values)
    second, third = split_high(rest)
    return tuple(part.astype(jnp.bfloat16) for part in (first, second, third))


def exact_dot(spec, values, onehot, values_first):
    stacked = jnp.stack(three_bf16(values), 0)
    left, right = spec.split("->")[0].split(",")
    output = spec.split("->")[1]
    if values_first:
        terms = jnp.einsum(
            "k" + left + "," + right + "->k" + output, stacked, onehot,
            preferred_element_type=jnp.float32,
        )
    else:
        terms = jnp.einsum(
            left + ",k" + right + "->k" + output, onehot, stacked,
            preferred_element_type=jnp.float32,
        )
    return terms[0] + terms[1] + terms[2]


def make_pack(tile_count, row_count, blocks, capacity):
    slot_total = blocks * capacity

    def pack_kernel(route_ref, length_ref, cell_ref, record_ref, out_ref, load_ref, plan_ref):
        tile_iota_row = lax.broadcasted_iota(jnp.int32, (tile_count, tile_count), 1)
        tile_iota_col = lax.broadcasted_iota(jnp.int32, (tile_count, tile_count), 0)
        diagonal = tile_iota_row == tile_iota_col
        target = jnp.sum(jnp.where(diagonal, route_ref[...], 0), axis=1, keepdims=True)
        lengths_col = jnp.sum(jnp.where(diagonal, length_ref[...], 0), axis=1, keepdims=True)
        block_hot = (
            target == lax.broadcasted_iota(jnp.int32, (tile_count, blocks), 1)
        ).astype(jnp.float32)
        same = lax.dot_general(
            block_hot, block_hot, (((1,), (1,)), ((), ())), preferred_element_type=jnp.float32
        )
        rank = jnp.sum(jnp.where(tile_iota_row < tile_iota_col, same, 0.0), axis=1, keepdims=True)
        slot = target * capacity + rank.astype(jnp.int32)
        slot_hot = (
            slot == lax.broadcasted_iota(jnp.int32, (tile_count, slot_total), 1)
        ).astype(jnp.float32)
        plan_ref[...] = slot_hot
        eye = (
            lax.broadcasted_iota(jnp.int32, (slot_total, slot_total), 0)
            == lax.broadcasted_iota(jnp.int32, (slot_total, slot_total), 1)
        ).astype(jnp.float32)
        plan = lax.dot_general(
            eye, slot_hot, (((1,), (1,)), ((), ())), preferred_element_type=jnp.float32
        )
        live = lax.broadcasted_iota(jnp.int32, (tile_count, row_count), 1) < lengths_col
        for comp in range(3):
            load_ref[comp] = jnp.where(live, record_ref[5 + comp], 0.0)
        for comp in range(6):
            if comp == 0:
                rows = jnp.abs(record_ref[0])
            elif comp < 5:
                rows = record_ref[comp]
            else:
                rows = jnp.where(live, cell_ref[...], -1).astype(jnp.float32)
            out_ref[:, comp * row_count:(comp + 1) * row_count] = jnp.dot(
                plan, rows, precision=lax.Precision.HIGHEST, preferred_element_type=jnp.float32
            )

    def pack(routes, lengths, cell_ids, records):
        return pl.pallas_call(
            pack_kernel,
            out_shape=(
                jax.ShapeDtypeStruct((slot_total, 6 * row_count), jnp.float32),
                jax.ShapeDtypeStruct((3, tile_count, row_count), jnp.float32),
                jax.ShapeDtypeStruct((tile_count, slot_total), jnp.float32),
            ),
        )(routes.reshape(1, tile_count), lengths.reshape(1, tile_count), cell_ids, records)
    return pack


def shards(density, momentum_energy, viscosity, records, cell_ids, routes, lengths):
    fluid_state = jnp.concatenate([density[None], momentum_energy], 0)
    cells_x, cells_y, vertical_cells = density.shape
    plane_count = cells_x * cells_y
    tile_count = records.shape[1]
    row_count = records.shape[2]
    blocks = lax.axis_size("stream") * lax.axis_size("cross")
    capacity = max(2, 2 * tile_count // blocks)
    slot_total = blocks * capacity
    faces = slot_total * row_count

    pack = make_pack(tile_count, row_count, blocks, capacity)
    outbound, load_rows, placement_plan = pack(routes, lengths, cell_ids, records)
    arrived = lax.all_to_all(outbound, ("stream", "cross"), split_axis=0, concat_axis=0, tiled=True)
    outbound, state_and_visc = lax.optimization_barrier(
        (outbound, jnp.concatenate([fluid_state, viscosity[None]], 0))
    )
    state_visc = face_halo(state_and_visc)
    state_pad = state_visc[0:5]
    visc_pad = state_visc[5]

    cells = jnp.round(arrived[:, 5 * row_count:]).astype(jnp.int32).reshape(faces)
    plane = cells // vertical_cells
    depth = cells % vertical_cells
    depth_hot = (
        depth[:, None] == lax.broadcasted_iota(jnp.int32, (faces, vertical_cells), 1)
    )
    plane_rows = plane[None, :] == lax.broadcasted_iota(jnp.int32, (plane_count, faces), 0)
    arrived_values = jnp.stack(
        [arrived[:, c * row_count:(c + 1) * row_count].reshape(faces) for c in range(5)], 0
    )
    spread = jnp.where(plane_rows[None], arrived_values[:, None, :], 0.0)
    source = jnp.einsum(
        "cpf,fd->cpd", spread, depth_hot.astype(jnp.float32), precision=lax.Precision.HIGH
    )
    source = source.reshape(5, cells_x, cells_y, vertical_cells)

    middle = shifted(state_pad, 1, 0, 0) + viscous(state_pad, visc_pad) + source
    middle_pad = face_halo(middle)
    new_state = middle + viscous(middle_pad, visc_pad)

    flat_state = new_state.reshape(5, plane_count, vertical_cells)
    kinetic = (
        flat_state[1] * flat_state[1]
        + flat_state[2] * flat_state[2]
        + flat_state[3] * flat_state[3]
    )
    pressure = 0.4 * (flat_state[4] - 0.5 * kinetic / flat_state[0])
    picked = exact_dot("fd,dp->fp", pressure.T, depth_hot.astype(jnp.bfloat16), False)
    plane_cols = plane[:, None] == lax.broadcasted_iota(jnp.int32, (faces, plane_count), 1)
    face_pressure = jnp.sum(jnp.where(plane_cols, picked, 0.0), axis=1)
    returned = lax.all_to_all(
        face_pressure.reshape(1, slot_total, row_count),
        ("stream", "cross"),
        split_axis=1,
        concat_axis=1,
        tiled=True,
    )
    home_pressure = jnp.einsum(
        "ts,sr->tr", placement_plan, returned[0], precision=lax.Precision.HIGHEST
    )
    face_loads = load_rows * home_pressure[None]
    return (new_state, face_loads)


def solution(mesh):
    placed = (
        P("stream", "cross", "gore"),
        P(None, "stream", "cross", "gore"),
        P("stream", "cross", "gore"),
        P(None, ("stream", "cross", "gore"), None),
        P(("stream", "cross", "gore"), None),
        P(("stream", "cross", "gore"), None),
        P(("stream", "cross", "gore")),
    )
    return jax.shard_map(
        shards,
        mesh=mesh,
        in_specs=placed,
        out_specs=(P(None, "stream", "cross", "gore"), P(None, ("stream", "cross", "gore"), None)),
        check_vma=False,
    )
```

```python
import jax
import jax.numpy as jnp
from jax import lax
from jax.experimental import pallas as pl
from jax.sharding import PartitionSpec as P


SIDES = (("stream", 1), ("cross", 2), ("gore", 3))


def face_halo(block):
    wide = block
    for axis, dim in SIDES:
        count = lax.axis_size(axis)
        index = lax.axis_index(axis)
        odd = index % 2 == 1
        extent = block.shape[dim]
        last = lax.slice_in_dim(block, extent - 1, None, axis=dim)
        first = lax.slice_in_dim(block, 0, 1, axis=dim)
        pairs_a = [(i, i ^ 1) for i in range(count) if (i ^ 1) < count]
        pairs_b = [(i, j) for i in range(1, count) for j in (i - 1, i + 1) if j >= 1 and j < count and (min(i, j) % 2 == 1)]
        from_a = lax.ppermute(jnp.where(odd, first, last), axis, pairs_a)
        if pairs_b:
            from_b = lax.ppermute(jnp.where(odd, last, first), axis, pairs_b)
        else:
            from_b = jnp.zeros_like(from_a)
        low = jnp.where(odd, from_a, from_b)
        high = jnp.where(odd, from_b, from_a)
        widths = [(0, 0)] + [(1, 1) if d < dim else (0, 0) for d in range(1, 4)]
        wide = jnp.concatenate([jnp.pad(low, widths), wide, jnp.pad(high, widths)], axis=dim)
    return wide


def harmonic(first_visc, second_visc):
    summed = first_visc + second_visc
    denominator = jnp.where(summed > 0, summed, 1.0)
    return 2.0 * first_visc * second_visc / denominator


def shifted(values, leading, spatial, offset):
    value_portions = [slice(None)] * leading
    for position in range(3):
        extent = values.shape[leading + position]
        if position == spatial:
            value_portions.append(slice(1 + offset, extent - 1 + offset))
        else:
            value_portions.append(slice(1, extent - 1))
    return values[tuple(value_portions)]


def viscous(field, visc):
    centre = shifted(field, 1, 0, 0)
    centre_visc = shifted(visc, 0, 0, 0)
    change = jnp.zeros_like(centre)
    for spatial in range(3):
        for offset in (1, -1):
            face_visc = harmonic(centre_visc, shifted(visc, 0, spatial, offset))
            change = change + face_visc[None] * (shifted(field, 1, spatial, offset) - centre)
    return change


def split_high(values):
    scaled = values * jnp.float32(65537.0)
    high = scaled - (scaled - values)
    return (high, values - high)


def three_bf16(values):
    first, rest = split_high(values)
    second, third = split_high(rest)
    return tuple(part.astype(jnp.bfloat16) for part in (first, second, third))


def exact_dot(spec, values, onehot, values_first):
    stacked = jnp.stack(three_bf16(values), 0)
    left, right = spec.split("->")[0].split(",")
    output = spec.split("->")[1]
    if values_first:
        terms = jnp.einsum(
            "k" + left + "," + right + "->k" + output, stacked, onehot,
            preferred_element_type=jnp.float32,
        )
    else:
        terms = jnp.einsum(
            left + ",k" + right + "->k" + output, onehot, stacked,
            preferred_element_type=jnp.float32,
        )
    return terms[0] + terms[1] + terms[2]


def make_pack(tile_count, row_count, blocks, capacity):
    slot_total = blocks * capacity

    def pack_kernel(route_ref, length_ref, cell_ref, record_ref, out_ref, load_ref, plan_ref):
        tile_iota_row = lax.broadcasted_iota(jnp.int32, (tile_count, tile_count), 1)
        tile_iota_col = lax.broadcasted_iota(jnp.int32, (tile_count, tile_count), 0)
        diagonal = tile_iota_row == tile_iota_col
        target = jnp.sum(jnp.where(diagonal, route_ref[...], 0), axis=1, keepdims=True)
        lengths_col = jnp.sum(jnp.where(diagonal, length_ref[...], 0), axis=1, keepdims=True)
        block_hot = (
            target == lax.broadcasted_iota(jnp.int32, (tile_count, blocks), 1)
        ).astype(jnp.float32)
        same = lax.dot_general(
            block_hot, block_hot, (((1,), (1,)), ((), ())), preferred_element_type=jnp.float32
        )
        rank = jnp.sum(jnp.where(tile_iota_row < tile_iota_col, same, 0.0), axis=1, keepdims=True)
        slot = target * capacity + rank.astype(jnp.int32)
        slot_hot = (
            slot == lax.broadcasted_iota(jnp.int32, (tile_count, slot_total), 1)
        ).astype(jnp.float32)
        plan_ref[...] = slot_hot
        eye = (
            lax.broadcasted_iota(jnp.int32, (slot_total, slot_total), 0)
            == lax.broadcasted_iota(jnp.int32, (slot_total, slot_total), 1)
        ).astype(jnp.float32)
        plan = lax.dot_general(
            eye, slot_hot, (((1,), (1,)), ((), ())), preferred_element_type=jnp.float32
        )
        plan_half = plan.astype(jnp.bfloat16)
        live = lax.broadcasted_iota(jnp.int32, (tile_count, row_count), 1) < lengths_col
        for comp in range(3):
            load_ref[comp] = jnp.where(live, record_ref[5 + comp], 0.0)
        for comp in range(6):
            if comp == 0:
                rows = jnp.abs(record_ref[0])
            elif comp < 5:
                rows = record_ref[comp]
            else:
                rows = jnp.where(live, cell_ref[...], -1).astype(jnp.float32)
            high, rest = split_high(rows)
            middle, low = split_high(rest)
            total = None
            for part in (high, middle, low):
                term = jnp.dot(
                    plan_half, part.astype(jnp.bfloat16), preferred_element_type=jnp.float32
                )
                total = term if total is None else total + term
            out_ref[:, comp * row_count:(comp + 1) * row_count] = total

    def pack(routes, lengths, cell_ids, records):
        return pl.pallas_call(
            pack_kernel,
            out_shape=(
                jax.ShapeDtypeStruct((slot_total, 6 * row_count), jnp.float32),
                jax.ShapeDtypeStruct((3, tile_count, row_count), jnp.float32),
                jax.ShapeDtypeStruct((tile_count, slot_total), jnp.float32),
            ),
        )(routes.reshape(1, tile_count), lengths.reshape(1, tile_count), cell_ids, records)
    return pack


def shards(density, momentum_energy, viscosity, records, cell_ids, routes, lengths):
    fluid_state = jnp.concatenate([density[None], momentum_energy], 0)
    cells_x, cells_y, vertical_cells = density.shape
    plane_count = cells_x * cells_y
    tile_count = records.shape[1]
    row_count = records.shape[2]
    blocks = lax.axis_size("stream") * lax.axis_size("cross")
    capacity = max(2, 2 * tile_count // blocks)
    slot_total = blocks * capacity
    faces = slot_total * row_count

    pack = make_pack(tile_count, row_count, blocks, capacity)
    outbound, load_rows, placement_plan = pack(routes, lengths, cell_ids, records)
    arrived = lax.all_to_all(outbound, ("stream", "cross"), split_axis=0, concat_axis=0, tiled=True)
    outbound, state_and_visc = lax.optimization_barrier(
        (outbound, jnp.concatenate([fluid_state, viscosity[None]], 0))
    )
    state_visc = face_halo(state_and_visc)
    state_pad = state_visc[0:5]
    visc_pad = state_visc[5]

    cells = jnp.round(arrived[:, 5 * row_count:]).astype(jnp.int32).reshape(faces)
    plane = cells // vertical_cells
    depth = cells % vertical_cells
    depth_hot = (
        depth[:, None] == lax.broadcasted_iota(jnp.int32, (faces, vertical_cells), 1)
    )
    plane_rows = plane[None, :] == lax.broadcasted_iota(jnp.int32, (plane_count, faces), 0)
    arrived_values = jnp.stack(
        [arrived[:, c * row_count:(c + 1) * row_count].reshape(faces) for c in range(5)], 0
    )
    spread = jnp.where(plane_rows[None], arrived_values[:, None, :], 0.0)
    source = jnp.einsum(
        "cpf,fd->cpd", spread, depth_hot.astype(jnp.float32), precision=lax.Precision.HIGH
    )
    source = source.reshape(5, cells_x, cells_y, vertical_cells)

    middle = shifted(state_pad, 1, 0, 0) + viscous(state_pad, visc_pad) + source
    middle_pad = face_halo(middle)
    new_state = middle + viscous(middle_pad, visc_pad)

    flat_state = new_state.reshape(5, plane_count, vertical_cells)
    kinetic = (
        flat_state[1] * flat_state[1]
        + flat_state[2] * flat_state[2]
        + flat_state[3] * flat_state[3]
    )
    pressure = 0.4 * (flat_state[4] - 0.5 * kinetic / flat_state[0])
    picked = exact_dot("fd,dp->fp", pressure.T, depth_hot.astype(jnp.bfloat16), False)
    plane_cols = plane[:, None] == lax.broadcasted_iota(jnp.int32, (faces, plane_count), 1)
    face_pressure = jnp.sum(jnp.where(plane_cols, picked, 0.0), axis=1)
    returned = lax.all_to_all(
        face_pressure.reshape(1, slot_total, row_count),
        ("stream", "cross"),
        split_axis=1,
        concat_axis=1,
        tiled=True,
    )
    home_pressure = jnp.einsum(
        "ts,sr->tr", placement_plan, returned[0], precision=lax.Precision.HIGHEST
    )
    face_loads = load_rows * home_pressure[None]
    return (new_state, face_loads)


def solution(mesh):
    placed = (
        P("stream", "cross", "gore"),
        P(None, "stream", "cross", "gore"),
        P("stream", "cross", "gore"),
        P(None, ("stream", "cross", "gore"), None),
        P(("stream", "cross", "gore"), None),
        P(("stream", "cross", "gore"), None),
        P(("stream", "cross", "gore")),
    )
    return jax.shard_map(
        shards,
        mesh=mesh,
        in_specs=placed,
        out_specs=(P(None, "stream", "cross", "gore"), P(None, ("stream", "cross", "gore"), None)),
        check_vma=False,
    )
```

```python
import jax
import jax.numpy as jnp
from jax import lax
from jax.experimental import pallas as pl
from jax.experimental.pallas import tpu as pltpu
from jax.sharding import PartitionSpec as P


SIDES = (("stream", 1), ("cross", 2), ("gore", 3))


def face_halo(block):
    wide = block
    for axis, dim in SIDES:
        count = lax.axis_size(axis)
        index = lax.axis_index(axis)
        odd = index % 2 == 1
        extent = block.shape[dim]
        last = lax.slice_in_dim(block, extent - 1, None, axis=dim)
        first = lax.slice_in_dim(block, 0, 1, axis=dim)
        pairs_a = [(i, i ^ 1) for i in range(count) if (i ^ 1) < count]
        pairs_b = [(i, j) for i in range(1, count) for j in (i - 1, i + 1) if j >= 1 and j < count and (min(i, j) % 2 == 1)]
        from_a = lax.ppermute(jnp.where(odd, first, last), axis, pairs_a)
        if pairs_b:
            from_b = lax.ppermute(jnp.where(odd, last, first), axis, pairs_b)
        else:
            from_b = jnp.zeros_like(from_a)
        low = jnp.where(odd, from_a, from_b)
        high = jnp.where(odd, from_b, from_a)
        widths = [(0, 0)] + [(1, 1) if d < dim else (0, 0) for d in range(1, 4)]
        wide = jnp.concatenate([jnp.pad(low, widths), wide, jnp.pad(high, widths)], axis=dim)
    return wide


def harmonic(first_visc, second_visc):
    summed = first_visc + second_visc
    denominator = jnp.where(summed > 0, summed, 1.0)
    return 2.0 * first_visc * second_visc / denominator


def shifted(values, leading, spatial, offset):
    value_portions = [slice(None)] * leading
    for position in range(3):
        extent = values.shape[leading + position]
        if position == spatial:
            value_portions.append(slice(1 + offset, extent - 1 + offset))
        else:
            value_portions.append(slice(1, extent - 1))
    return values[tuple(value_portions)]


def viscous(field, visc):
    centre = shifted(field, 1, 0, 0)
    centre_visc = shifted(visc, 0, 0, 0)
    change = jnp.zeros_like(centre)
    for spatial in range(3):
        for offset in (1, -1):
            face_visc = harmonic(centre_visc, shifted(visc, 0, spatial, offset))
            change = change + face_visc[None] * (shifted(field, 1, spatial, offset) - centre)
    return change


def split_high(values):
    scaled = values * jnp.float32(65537.0)
    high = scaled - (scaled - values)
    return (high, values - high)


def three_bf16(values):
    first, rest = split_high(values)
    second, third = split_high(rest)
    return tuple(part.astype(jnp.bfloat16) for part in (first, second, third))


def exact_dot(spec, values, onehot, values_first):
    stacked = jnp.stack(three_bf16(values), 0)
    left, right = spec.split("->")[0].split(",")
    output = spec.split("->")[1]
    if values_first:
        terms = jnp.einsum(
            "k" + left + "," + right + "->k" + output, stacked, onehot,
            preferred_element_type=jnp.float32,
        )
    else:
        terms = jnp.einsum(
            left + ",k" + right + "->k" + output, onehot, stacked,
            preferred_element_type=jnp.float32,
        )
    return terms[0] + terms[1] + terms[2]


def make_pack(tile_count, row_count, blocks, capacity):
    slot_total = blocks * capacity

    def pack_kernel(route_ref, length_ref, cell_ref, record_ref, out_ref, load_ref, plan_ref):
        tile_iota_row = lax.broadcasted_iota(jnp.int32, (tile_count, tile_count), 1)
        tile_iota_col = lax.broadcasted_iota(jnp.int32, (tile_count, tile_count), 0)
        diagonal = tile_iota_row == tile_iota_col
        target = jnp.sum(jnp.where(diagonal, route_ref[...], 0), axis=1, keepdims=True)
        lengths_col = jnp.sum(jnp.where(diagonal, length_ref[...], 0), axis=1, keepdims=True)
        block_hot = (
            target == lax.broadcasted_iota(jnp.int32, (tile_count, blocks), 1)
        ).astype(jnp.float32)
        same = lax.dot_general(
            block_hot, block_hot, (((1,), (1,)), ((), ())), preferred_element_type=jnp.float32
        )
        rank = jnp.sum(jnp.where(tile_iota_row < tile_iota_col, same, 0.0), axis=1, keepdims=True)
        slot = target * capacity + rank.astype(jnp.int32)
        slot_hot = (
            slot == lax.broadcasted_iota(jnp.int32, (tile_count, slot_total), 1)
        ).astype(jnp.float32)
        plan_ref[...] = slot_hot
        eye = (
            lax.broadcasted_iota(jnp.int32, (slot_total, slot_total), 0)
            == lax.broadcasted_iota(jnp.int32, (slot_total, slot_total), 1)
        ).astype(jnp.float32)
        plan = lax.dot_general(
            eye, slot_hot, (((1,), (1,)), ((), ())), preferred_element_type=jnp.float32
        )
        plan_half = plan.astype(jnp.bfloat16)
        live = lax.broadcasted_iota(jnp.int32, (tile_count, row_count), 1) < lengths_col
        for comp in range(3):
            load_ref[comp] = jnp.where(live, record_ref[5 + comp], 0.0)
        for comp in range(6):
            if comp == 0:
                rows = jnp.abs(record_ref[0])
            elif comp < 5:
                rows = record_ref[comp]
            else:
                rows = jnp.where(live, cell_ref[...], -1).astype(jnp.float32)
            high, rest = split_high(rows)
            middle, low = split_high(rest)
            total = None
            for part in (high, middle, low):
                term = jnp.dot(
                    plan_half, part.astype(jnp.bfloat16), preferred_element_type=jnp.float32
                )
                total = term if total is None else total + term
            out_ref[:, comp * row_count:(comp + 1) * row_count] = total

    def pack(routes, lengths, cell_ids, records):
        return pl.pallas_call(
            pack_kernel,
            out_shape=(
                jax.ShapeDtypeStruct((slot_total, 6 * row_count), jnp.float32),
                jax.ShapeDtypeStruct((3, tile_count, row_count), jnp.float32),
                jax.ShapeDtypeStruct((tile_count, slot_total), jnp.float32),
            ),
        )(routes.reshape(1, tile_count), lengths.reshape(1, tile_count), cell_ids, records)
    return pack


def make_source(slot_total, row_count, plane_count, vertical_cells):
    group = 8
    width = group * row_count
    rows_out = 15 * plane_count

    def source_kernel(arrived_ref, out_ref, left_ref, right_ref):
        out_ref[...] = jnp.zeros_like(out_ref)
        depth_iota = lax.broadcasted_iota(jnp.int32, (vertical_cells, row_count), 0).astype(jnp.float32)
        plane_iota = lax.broadcasted_iota(jnp.int32, (plane_count, row_count), 0).astype(jnp.float32)

        def body(step, carry):
            block = arrived_ref[pl.ds(pl.multiple_of(step * group, group), group), :]
            for g in range(group):
                row = block[g:g + 1, :]
                cell = row[:, 5 * row_count:6 * row_count]
                plane = jnp.floor((cell + 0.5) / vertical_cells)
                depth = cell - plane * vertical_cells
                lanes = slice(g * row_count, (g + 1) * row_count)
                right_ref[:, lanes] = (depth_iota == depth).astype(jnp.bfloat16)
                hit = plane_iota == plane
                for comp in range(5):
                    spread = jnp.where(hit, row[:, comp * row_count:(comp + 1) * row_count], 0.0)
                    high, rest = split_high(spread)
                    middle, low = split_high(rest)
                    for piece, part in enumerate((high, middle, low)):
                        start = (piece * 5 + comp) * plane_count
                        left_ref[start:start + plane_count, lanes] = part.astype(jnp.bfloat16)
            out_ref[...] += lax.dot_general(
                left_ref[...], right_ref[...], (((1,), (1,)), ((), ())),
                preferred_element_type=jnp.float32,
            )
            return carry

        lax.fori_loop(0, slot_total // group, body, 0)

    def source(arrived):
        total = pl.pallas_call(
            source_kernel,
            out_shape=jax.ShapeDtypeStruct((rows_out, vertical_cells), jnp.float32),
            scratch_shapes=[
                pltpu.VMEM((rows_out, width), jnp.bfloat16),
                pltpu.VMEM((vertical_cells, width), jnp.bfloat16),
            ],
        )(arrived)
        third = 5 * plane_count
        return total[0:third] + total[third:2 * third] + total[2 * third:]
    return source


def shards(density, momentum_energy, viscosity, records, cell_ids, routes, lengths):
    fluid_state = jnp.concatenate([density[None], momentum_energy], 0)
    cells_x, cells_y, vertical_cells = density.shape
    plane_count = cells_x * cells_y
    tile_count = records.shape[1]
    row_count = records.shape[2]
    blocks = lax.axis_size("stream") * lax.axis_size("cross")
    capacity = max(2, 2 * tile_count // blocks)
    slot_total = blocks * capacity
    faces = slot_total * row_count

    pack = make_pack(tile_count, row_count, blocks, capacity)
    outbound, load_rows, placement_plan = pack(routes, lengths, cell_ids, records)
    arrived = lax.all_to_all(outbound, ("stream", "cross"), split_axis=0, concat_axis=0, tiled=True)
    outbound, state_and_visc = lax.optimization_barrier(
        (outbound, jnp.concatenate([fluid_state, viscosity[None]], 0))
    )
    state_visc = face_halo(state_and_visc)
    state_pad = state_visc[0:5]
    visc_pad = state_visc[5]

    cells = jnp.round(arrived[:, 5 * row_count:]).astype(jnp.int32).reshape(faces)
    plane = cells // vertical_cells
    depth = cells % vertical_cells
    depth_hot = (
        depth[:, None] == lax.broadcasted_iota(jnp.int32, (faces, vertical_cells), 1)
    )
    source = make_source(slot_total, row_count, plane_count, vertical_cells)(arrived)
    source = source.reshape(5, cells_x, cells_y, vertical_cells)

    middle = shifted(state_pad, 1, 0, 0) + viscous(state_pad, visc_pad) + source
    middle_pad = face_halo(middle)
    new_state = middle + viscous(middle_pad, visc_pad)

    flat_state = new_state.reshape(5, plane_count, vertical_cells)
    kinetic = (
        flat_state[1] * flat_state[1]
        + flat_state[2] * flat_state[2]
        + flat_state[3] * flat_state[3]
    )
    pressure = 0.4 * (flat_state[4] - 0.5 * kinetic / flat_state[0])
    picked = exact_dot("fd,dp->fp", pressure.T, depth_hot.astype(jnp.bfloat16), False)
    plane_cols = plane[:, None] == lax.broadcasted_iota(jnp.int32, (faces, plane_count), 1)
    face_pressure = jnp.sum(jnp.where(plane_cols, picked, 0.0), axis=1)
    returned = lax.all_to_all(
        face_pressure.reshape(1, slot_total, row_count),
        ("stream", "cross"),
        split_axis=1,
        concat_axis=1,
        tiled=True,
    )
    home_pressure = jnp.einsum(
        "ts,sr->tr", placement_plan, returned[0], precision=lax.Precision.HIGHEST
    )
    face_loads = load_rows * home_pressure[None]
    return (new_state, face_loads)


def solution(mesh):
    placed = (
        P("stream", "cross", "gore"),
        P(None, "stream", "cross", "gore"),
        P("stream", "cross", "gore"),
        P(None, ("stream", "cross", "gore"), None),
        P(("stream", "cross", "gore"), None),
        P(("stream", "cross", "gore"), None),
        P(("stream", "cross", "gore")),
    )
    return jax.shard_map(
        shards,
        mesh=mesh,
        in_specs=placed,
        out_specs=(P(None, "stream", "cross", "gore"), P(None, ("stream", "cross", "gore"), None)),
        check_vma=False,
    )
```

```python
import jax
import jax.numpy as jnp
from jax import lax
from jax.experimental import pallas as pl
from jax.sharding import PartitionSpec as P


SIDES = (("stream", 1), ("cross", 2), ("gore", 3))


def face_halo(block):
    wide = block
    for axis, dim in SIDES:
        count = lax.axis_size(axis)
        index = lax.axis_index(axis)
        odd = index % 2 == 1
        extent = block.shape[dim]
        last = lax.slice_in_dim(block, extent - 1, None, axis=dim)
        first = lax.slice_in_dim(block, 0, 1, axis=dim)
        pairs_a = [(i, i ^ 1) for i in range(count) if (i ^ 1) < count]
        pairs_b = [(i, j) for i in range(1, count) for j in (i - 1, i + 1) if j >= 1 and j < count and (min(i, j) % 2 == 1)]
        from_a = lax.ppermute(jnp.where(odd, first, last), axis, pairs_a)
        if pairs_b:
            from_b = lax.ppermute(jnp.where(odd, last, first), axis, pairs_b)
        else:
            from_b = jnp.zeros_like(from_a)
        low = jnp.where(odd, from_a, from_b)
        high = jnp.where(odd, from_b, from_a)
        widths = [(0, 0)] + [(1, 1) if d < dim else (0, 0) for d in range(1, 4)]
        wide = jnp.concatenate([jnp.pad(low, widths), wide, jnp.pad(high, widths)], axis=dim)
    return wide


def harmonic(first_visc, second_visc):
    summed = first_visc + second_visc
    denominator = jnp.where(summed > 0, summed, 1.0)
    return 2.0 * first_visc * second_visc / denominator


def shifted(values, leading, spatial, offset):
    value_portions = [slice(None)] * leading
    for position in range(3):
        extent = values.shape[leading + position]
        if position == spatial:
            value_portions.append(slice(1 + offset, extent - 1 + offset))
        else:
            value_portions.append(slice(1, extent - 1))
    return values[tuple(value_portions)]


def viscous(field, visc):
    centre = shifted(field, 1, 0, 0)
    centre_visc = shifted(visc, 0, 0, 0)
    change = jnp.zeros_like(centre)
    for spatial in range(3):
        for offset in (1, -1):
            face_visc = harmonic(centre_visc, shifted(visc, 0, spatial, offset))
            change = change + face_visc[None] * (shifted(field, 1, spatial, offset) - centre)
    return change


def split_high(values):
    scaled = values * jnp.float32(65537.0)
    high = scaled - (scaled - values)
    return (high, values - high)


def exact_dot(spec, values, onehot, values_first):
    high, rest = split_high(values)
    stacked = jnp.stack([high.astype(jnp.bfloat16), rest.astype(jnp.bfloat16)], 0)
    left, right = spec.split("->")[0].split(",")
    output = spec.split("->")[1]
    if values_first:
        terms = jnp.einsum(
            "k" + left + "," + right + "->k" + output, stacked, onehot,
            preferred_element_type=jnp.float32,
        )
    else:
        terms = jnp.einsum(
            left + ",k" + right + "->k" + output, onehot, stacked,
            preferred_element_type=jnp.float32,
        )
    return terms[0] + terms[1]


def make_pack(tile_count, row_count, blocks, capacity):
    slot_total = blocks * capacity

    def pack_kernel(route_ref, length_ref, cell_ref, record_ref, out_ref, load_ref, plan_ref):
        tile_iota_row = lax.broadcasted_iota(jnp.int32, (tile_count, tile_count), 1)
        tile_iota_col = lax.broadcasted_iota(jnp.int32, (tile_count, tile_count), 0)
        diagonal = tile_iota_row == tile_iota_col
        target = jnp.sum(jnp.where(diagonal, route_ref[...], 0), axis=1, keepdims=True)
        lengths_col = jnp.sum(jnp.where(diagonal, length_ref[...], 0), axis=1, keepdims=True)
        block_hot = (
            target == lax.broadcasted_iota(jnp.int32, (tile_count, blocks), 1)
        ).astype(jnp.float32)
        same = lax.dot_general(
            block_hot, block_hot, (((1,), (1,)), ((), ())), preferred_element_type=jnp.float32
        )
        rank = jnp.sum(jnp.where(tile_iota_row < tile_iota_col, same, 0.0), axis=1, keepdims=True)
        slot = target * capacity + rank.astype(jnp.int32)
        slot_hot = (
            slot == lax.broadcasted_iota(jnp.int32, (tile_count, slot_total), 1)
        ).astype(jnp.float32)
        plan_ref[...] = slot_hot
        eye = (
            lax.broadcasted_iota(jnp.int32, (slot_total, slot_total), 0)
            == lax.broadcasted_iota(jnp.int32, (slot_total, slot_total), 1)
        ).astype(jnp.float32)
        plan = lax.dot_general(
            eye, slot_hot, (((1,), (1,)), ((), ())), preferred_element_type=jnp.float32
        )
        plan_half = plan.astype(jnp.bfloat16)
        live = lax.broadcasted_iota(jnp.int32, (tile_count, row_count), 1) < lengths_col
        for comp in range(3):
            load_ref[comp] = jnp.where(live, record_ref[5 + comp], 0.0)
        for comp in range(6):
            if comp == 0:
                rows = jnp.abs(record_ref[0])
            elif comp < 5:
                rows = record_ref[comp]
            else:
                rows = jnp.where(live, cell_ref[...], -1).astype(jnp.float32)
            high, rest = split_high(rows)
            middle, low = split_high(rest)
            total = None
            for part in (high, middle, low):
                term = jnp.dot(
                    plan_half, part.astype(jnp.bfloat16), preferred_element_type=jnp.float32
                )
                total = term if total is None else total + term
            out_ref[:, comp * row_count:(comp + 1) * row_count] = total

    def pack(routes, lengths, cell_ids, records):
        return pl.pallas_call(
            pack_kernel,
            out_shape=(
                jax.ShapeDtypeStruct((slot_total, 6 * row_count), jnp.float32),
                jax.ShapeDtypeStruct((3, tile_count, row_count), jnp.float32),
                jax.ShapeDtypeStruct((tile_count, slot_total), jnp.float32),
            ),
        )(routes.reshape(1, tile_count), lengths.reshape(1, tile_count), cell_ids, records)
    return pack


def shards(density, momentum_energy, viscosity, records, cell_ids, routes, lengths):
    fluid_state = jnp.concatenate([density[None], momentum_energy], 0)
    cells_x, cells_y, vertical_cells = density.shape
    plane_count = cells_x * cells_y
    tile_count = records.shape[1]
    row_count = records.shape[2]
    blocks = lax.axis_size("stream") * lax.axis_size("cross")
    capacity = max(2, 2 * tile_count // blocks)
    slot_total = blocks * capacity
    faces = slot_total * row_count

    pack = make_pack(tile_count, row_count, blocks, capacity)
    outbound, load_rows, placement_plan = pack(routes, lengths, cell_ids, records)
    arrived = lax.all_to_all(outbound, ("stream", "cross"), split_axis=0, concat_axis=0, tiled=True)
    outbound, state_and_visc = lax.optimization_barrier(
        (outbound, jnp.concatenate([fluid_state, viscosity[None]], 0))
    )
    state_visc = face_halo(state_and_visc)
    state_pad = state_visc[0:5]
    visc_pad = state_visc[5]

    cells = jnp.round(arrived[:, 5 * row_count:]).astype(jnp.int32).reshape(faces)
    plane = cells // vertical_cells
    depth = cells % vertical_cells
    depth_hot = (
        depth[:, None] == lax.broadcasted_iota(jnp.int32, (faces, vertical_cells), 1)
    )
    plane_rows = plane[None, :] == lax.broadcasted_iota(jnp.int32, (plane_count, faces), 0)
    arrived_values = jnp.stack(
        [arrived[:, c * row_count:(c + 1) * row_count].reshape(faces) for c in range(5)], 0
    )
    spread = jnp.where(plane_rows[None], arrived_values[:, None, :], 0.0)
    source = jnp.einsum(
        "cpf,fd->cpd", spread, depth_hot.astype(jnp.float32), precision=lax.Precision.HIGH
    )
    source = source.reshape(5, cells_x, cells_y, vertical_cells)

    middle = shifted(state_pad, 1, 0, 0) + viscous(state_pad, visc_pad) + source
    middle_pad = face_halo(middle)
    new_state = middle + viscous(middle_pad, visc_pad)

    flat_state = new_state.reshape(5, plane_count, vertical_cells)
    kinetic = (
        flat_state[1] * flat_state[1]
        + flat_state[2] * flat_state[2]
        + flat_state[3] * flat_state[3]
    )
    pressure = 0.4 * (flat_state[4] - 0.5 * kinetic / flat_state[0])
    picked = exact_dot("fd,dp->fp", pressure.T, depth_hot.astype(jnp.bfloat16), False)
    plane_cols = plane[:, None] == lax.broadcasted_iota(jnp.int32, (faces, plane_count), 1)
    face_pressure = jnp.sum(jnp.where(plane_cols, picked, 0.0), axis=1)
    returned = lax.all_to_all(
        face_pressure.reshape(1, slot_total, row_count),
        ("stream", "cross"),
        split_axis=1,
        concat_axis=1,
        tiled=True,
    )
    home_pressure = jnp.einsum(
        "ts,sr->tr", placement_plan, returned[0], precision=lax.Precision.HIGHEST
    )
    face_loads = load_rows * home_pressure[None]
    return (new_state, face_loads)


def solution(mesh):
    placed = (
        P("stream", "cross", "gore"),
        P(None, "stream", "cross", "gore"),
        P("stream", "cross", "gore"),
        P(None, ("stream", "cross", "gore"), None),
        P(("stream", "cross", "gore"), None),
        P(("stream", "cross", "gore"), None),
        P(("stream", "cross", "gore")),
    )
    return jax.shard_map(
        shards,
        mesh=mesh,
        in_specs=placed,
        out_specs=(P(None, "stream", "cross", "gore"), P(None, ("stream", "cross", "gore"), None)),
        check_vma=False,
    )
```

```python
import jax
import jax.numpy as jnp
from jax import lax
from jax.experimental import pallas as pl
from jax.sharding import PartitionSpec as P


SIDES = (("stream", 1), ("cross", 2), ("gore", 3))


def face_halo(block, parts=None):
    parts = [block] if parts is None else parts
    wide = block
    for axis, dim in SIDES:
        count = lax.axis_size(axis)
        index = lax.axis_index(axis)
        odd = index % 2 == 1
        last = jnp.concatenate(
            [lax.slice_in_dim(part, part.shape[dim] - 1, None, axis=dim) for part in parts], 0
        )
        first = jnp.concatenate([lax.slice_in_dim(part, 0, 1, axis=dim) for part in parts], 0)
        pairs_a = [(i, i ^ 1) for i in range(count) if (i ^ 1) < count]
        pairs_b = [(i, j) for i in range(1, count) for j in (i - 1, i + 1) if j >= 1 and j < count and (min(i, j) % 2 == 1)]
        from_a = lax.ppermute(jnp.where(odd, first, last), axis, pairs_a)
        if pairs_b:
            from_b = lax.ppermute(jnp.where(odd, last, first), axis, pairs_b)
        else:
            from_b = jnp.zeros_like(from_a)
        low = jnp.where(odd, from_a, from_b)
        high = jnp.where(odd, from_b, from_a)
        widths = [(0, 0)] + [(1, 1) if d < dim else (0, 0) for d in range(1, 4)]
        wide = jnp.concatenate([jnp.pad(low, widths), wide, jnp.pad(high, widths)], axis=dim)
    return wide


def harmonic(first_visc, second_visc):
    summed = first_visc + second_visc
    denominator = jnp.where(summed > 0, summed, 1.0)
    return 2.0 * first_visc * second_visc / denominator


def shifted(values, leading, spatial, offset):
    value_portions = [slice(None)] * leading
    for position in range(3):
        extent = values.shape[leading + position]
        if position == spatial:
            value_portions.append(slice(1 + offset, extent - 1 + offset))
        else:
            value_portions.append(slice(1, extent - 1))
    return values[tuple(value_portions)]


def viscous(field, visc):
    centre = shifted(field, 1, 0, 0)
    centre_visc = shifted(visc, 0, 0, 0)
    change = jnp.zeros_like(centre)
    for spatial in range(3):
        for offset in (1, -1):
            face_visc = harmonic(centre_visc, shifted(visc, 0, spatial, offset))
            change = change + face_visc[None] * (shifted(field, 1, spatial, offset) - centre)
    return change


def split_high(values):
    scaled = values * jnp.float32(65537.0)
    high = scaled - (scaled - values)
    return (high, values - high)


def three_bf16(values):
    first, rest = split_high(values)
    second, third = split_high(rest)
    return tuple(part.astype(jnp.bfloat16) for part in (first, second, third))


def exact_dot(spec, values, onehot, values_first):
    stacked = jnp.stack(three_bf16(values), 0)
    left, right = spec.split("->")[0].split(",")
    output = spec.split("->")[1]
    if values_first:
        terms = jnp.einsum(
            "k" + left + "," + right + "->k" + output, stacked, onehot,
            preferred_element_type=jnp.float32,
        )
    else:
        terms = jnp.einsum(
            left + ",k" + right + "->k" + output, onehot, stacked,
            preferred_element_type=jnp.float32,
        )
    return terms[0] + terms[1] + terms[2]


def make_pack(tile_count, row_count, blocks, capacity):
    slot_total = blocks * capacity

    def pack_kernel(route_ref, length_ref, cell_ref, record_ref, out_ref, load_ref, plan_ref):
        tile_iota_row = lax.broadcasted_iota(jnp.int32, (tile_count, tile_count), 1)
        tile_iota_col = lax.broadcasted_iota(jnp.int32, (tile_count, tile_count), 0)
        diagonal = tile_iota_row == tile_iota_col
        target = jnp.sum(jnp.where(diagonal, route_ref[...], 0), axis=1, keepdims=True)
        lengths_col = jnp.sum(jnp.where(diagonal, length_ref[...], 0), axis=1, keepdims=True)
        block_hot = (
            target == lax.broadcasted_iota(jnp.int32, (tile_count, blocks), 1)
        ).astype(jnp.float32)
        same = lax.dot_general(
            block_hot, block_hot, (((1,), (1,)), ((), ())), preferred_element_type=jnp.float32
        )
        rank = jnp.sum(jnp.where(tile_iota_row < tile_iota_col, same, 0.0), axis=1, keepdims=True)
        slot = target * capacity + rank.astype(jnp.int32)
        slot_hot = (
            slot == lax.broadcasted_iota(jnp.int32, (tile_count, slot_total), 1)
        ).astype(jnp.float32)
        plan_ref[...] = slot_hot
        eye = (
            lax.broadcasted_iota(jnp.int32, (slot_total, slot_total), 0)
            == lax.broadcasted_iota(jnp.int32, (slot_total, slot_total), 1)
        ).astype(jnp.float32)
        plan = lax.dot_general(
            eye, slot_hot, (((1,), (1,)), ((), ())), preferred_element_type=jnp.float32
        )
        plan_half = plan.astype(jnp.bfloat16)
        live = lax.broadcasted_iota(jnp.int32, (tile_count, row_count), 1) < lengths_col
        for comp in range(3):
            load_ref[comp] = jnp.where(live, record_ref[5 + comp], 0.0)
        for comp in range(6):
            if comp == 0:
                rows = jnp.abs(record_ref[0])
            elif comp < 5:
                rows = record_ref[comp]
            else:
                rows = jnp.where(live, cell_ref[...], -1).astype(jnp.float32)
            high, rest = split_high(rows)
            middle, low = split_high(rest)
            total = None
            for part in (high, middle, low):
                term = jnp.dot(
                    plan_half, part.astype(jnp.bfloat16), preferred_element_type=jnp.float32
                )
                total = term if total is None else total + term
            out_ref[:, comp * row_count:(comp + 1) * row_count] = total

    def pack(routes, lengths, cell_ids, records):
        return pl.pallas_call(
            pack_kernel,
            out_shape=(
                jax.ShapeDtypeStruct((slot_total, 6 * row_count), jnp.float32),
                jax.ShapeDtypeStruct((3, tile_count, row_count), jnp.float32),
                jax.ShapeDtypeStruct((tile_count, slot_total), jnp.float32),
            ),
        )(routes.reshape(1, tile_count), lengths.reshape(1, tile_count), cell_ids, records)
    return pack


def shards(density, momentum_energy, viscosity, records, cell_ids, routes, lengths):
    fluid_state = jnp.concatenate([density[None], momentum_energy], 0)
    cells_x, cells_y, vertical_cells = density.shape
    plane_count = cells_x * cells_y
    tile_count = records.shape[1]
    row_count = records.shape[2]
    blocks = lax.axis_size("stream") * lax.axis_size("cross")
    capacity = max(2, 2 * tile_count // blocks)
    slot_total = blocks * capacity
    faces = slot_total * row_count

    pack = make_pack(tile_count, row_count, blocks, capacity)
    outbound, load_rows, placement_plan = pack(routes, lengths, cell_ids, records)
    arrived = lax.all_to_all(outbound, ("stream", "cross"), split_axis=0, concat_axis=0, tiled=True)
    outbound, density, momentum_energy, viscosity = lax.optimization_barrier(
        (outbound, density, momentum_energy, viscosity)
    )
    state_visc = face_halo(
        jnp.concatenate([density[None], momentum_energy, viscosity[None]], 0),
        [density[None], momentum_energy, viscosity[None]],
    )
    state_pad = state_visc[0:5]
    visc_pad = state_visc[5]

    cells = jnp.round(arrived[:, 5 * row_count:]).astype(jnp.int32).reshape(faces)
    plane = cells // vertical_cells
    depth = cells % vertical_cells
    depth_hot = (
        depth[:, None] == lax.broadcasted_iota(jnp.int32, (faces, vertical_cells), 1)
    )
    plane_rows = plane[None, :] == lax.broadcasted_iota(jnp.int32, (plane_count, faces), 0)
    arrived_values = jnp.stack(
        [arrived[:, c * row_count:(c + 1) * row_count].reshape(faces) for c in range(5)], 0
    )
    spread = jnp.where(plane_rows[None], arrived_values[:, None, :], 0.0)
    source = jnp.einsum(
        "cpf,fd->cpd", spread, depth_hot.astype(jnp.float32), precision=lax.Precision.HIGH
    )
    source = source.reshape(5, cells_x, cells_y, vertical_cells)

    middle = shifted(state_pad, 1, 0, 0) + viscous(state_pad, visc_pad) + source
    middle_pad = face_halo(middle)
    new_state = middle + viscous(middle_pad, visc_pad)

    flat_state = new_state.reshape(5, plane_count, vertical_cells)
    kinetic = (
        flat_state[1] * flat_state[1]
        + flat_state[2] * flat_state[2]
        + flat_state[3] * flat_state[3]
    )
    pressure = 0.4 * (flat_state[4] - 0.5 * kinetic / flat_state[0])
    picked = exact_dot("fd,dp->fp", pressure.T, depth_hot.astype(jnp.bfloat16), False)
    plane_cols = plane[:, None] == lax.broadcasted_iota(jnp.int32, (faces, plane_count), 1)
    face_pressure = jnp.sum(jnp.where(plane_cols, picked, 0.0), axis=1)
    returned = lax.all_to_all(
        face_pressure.reshape(1, slot_total, row_count),
        ("stream", "cross"),
        split_axis=1,
        concat_axis=1,
        tiled=True,
    )
    home_pressure = jnp.einsum(
        "ts,sr->tr", placement_plan, returned[0], precision=lax.Precision.HIGHEST
    )
    face_loads = load_rows * home_pressure[None]
    return (new_state, face_loads)


def solution(mesh):
    placed = (
        P("stream", "cross", "gore"),
        P(None, "stream", "cross", "gore"),
        P("stream", "cross", "gore"),
        P(None, ("stream", "cross", "gore"), None),
        P(("stream", "cross", "gore"), None),
        P(("stream", "cross", "gore"), None),
        P(("stream", "cross", "gore")),
    )
    return jax.shard_map(
        shards,
        mesh=mesh,
        in_specs=placed,
        out_specs=(P(None, "stream", "cross", "gore"), P(None, ("stream", "cross", "gore"), None)),
        check_vma=False,
    )
```

```python
import jax
import jax.numpy as jnp
from jax import lax
from jax.experimental import pallas as pl
from jax.sharding import PartitionSpec as P


SIDES = (("stream", 1), ("cross", 2), ("gore", 3))


def face_halo(block):
    wide = block
    for axis, dim in SIDES:
        count = lax.axis_size(axis)
        index = lax.axis_index(axis)
        odd = index % 2 == 1
        extent = block.shape[dim]
        last = lax.slice_in_dim(block, extent - 1, None, axis=dim)
        first = lax.slice_in_dim(block, 0, 1, axis=dim)
        pairs_a = [(i, i ^ 1) for i in range(count) if (i ^ 1) < count]
        pairs_b = [(i, j) for i in range(1, count) for j in (i - 1, i + 1) if j >= 1 and j < count and (min(i, j) % 2 == 1)]
        from_a = lax.ppermute(jnp.where(odd, first, last), axis, pairs_a)
        if pairs_b:
            from_b = lax.ppermute(jnp.where(odd, last, first), axis, pairs_b)
        else:
            from_b = jnp.zeros_like(from_a)
        low = jnp.where(odd, from_a, from_b)
        high = jnp.where(odd, from_b, from_a)
        widths = [(0, 0)] + [(1, 1) if d < dim else (0, 0) for d in range(1, 4)]
        wide = jnp.concatenate([jnp.pad(low, widths), wide, jnp.pad(high, widths)], axis=dim)
    return wide


def harmonic(first_visc, second_visc):
    summed = first_visc + second_visc
    denominator = jnp.where(summed > 0, summed, 1.0)
    return 2.0 * first_visc * second_visc / denominator


def shifted(values, leading, spatial, offset):
    value_portions = [slice(None)] * leading
    for position in range(3):
        extent = values.shape[leading + position]
        if position == spatial:
            value_portions.append(slice(1 + offset, extent - 1 + offset))
        else:
            value_portions.append(slice(1, extent - 1))
    return values[tuple(value_portions)]


def viscous(field, visc):
    centre = shifted(field, 1, 0, 0)
    centre_visc = shifted(visc, 0, 0, 0)
    change = jnp.zeros_like(centre)
    for spatial in range(3):
        for offset in (1, -1):
            face_visc = harmonic(centre_visc, shifted(visc, 0, spatial, offset))
            change = change + face_visc[None] * (shifted(field, 1, spatial, offset) - centre)
    return change


def split_high(values):
    scaled = values * jnp.float32(65537.0)
    high = scaled - (scaled - values)
    return (high, values - high)


def three_bf16(values):
    first, rest = split_high(values)
    second, third = split_high(rest)
    return tuple(part.astype(jnp.bfloat16) for part in (first, second, third))


def exact_dot(spec, values, onehot, values_first):
    stacked = jnp.stack(three_bf16(values), 0)
    left, right = spec.split("->")[0].split(",")
    output = spec.split("->")[1]
    if values_first:
        terms = jnp.einsum(
            "k" + left + "," + right + "->k" + output, stacked, onehot,
            preferred_element_type=jnp.float32,
        )
    else:
        terms = jnp.einsum(
            left + ",k" + right + "->k" + output, onehot, stacked,
            preferred_element_type=jnp.float32,
        )
    return terms[0] + terms[1] + terms[2]


def make_pack(tile_count, row_count, blocks, capacity):
    slot_total = blocks * capacity

    def pack_kernel(route_ref, length_ref, cell_ref, record_ref, out_ref, load_ref, plan_ref):
        tile_iota_row = lax.broadcasted_iota(jnp.int32, (tile_count, tile_count), 1)
        tile_iota_col = lax.broadcasted_iota(jnp.int32, (tile_count, tile_count), 0)
        diagonal = tile_iota_row == tile_iota_col
        target = jnp.sum(jnp.where(diagonal, route_ref[...], 0), axis=1, keepdims=True)
        lengths_col = jnp.sum(jnp.where(diagonal, length_ref[...], 0), axis=1, keepdims=True)
        block_hot = (
            target == lax.broadcasted_iota(jnp.int32, (tile_count, blocks), 1)
        ).astype(jnp.float32)
        same = lax.dot_general(
            block_hot, block_hot, (((1,), (1,)), ((), ())), preferred_element_type=jnp.float32
        )
        rank = jnp.sum(jnp.where(tile_iota_row < tile_iota_col, same, 0.0), axis=1, keepdims=True)
        slot = target * capacity + rank.astype(jnp.int32)
        slot_hot = (
            slot == lax.broadcasted_iota(jnp.int32, (tile_count, slot_total), 1)
        ).astype(jnp.float32)
        plan_ref[...] = slot_hot
        eye = (
            lax.broadcasted_iota(jnp.int32, (slot_total, slot_total), 0)
            == lax.broadcasted_iota(jnp.int32, (slot_total, slot_total), 1)
        ).astype(jnp.float32)
        plan = lax.dot_general(
            eye, slot_hot, (((1,), (1,)), ((), ())), preferred_element_type=jnp.float32
        )
        plan_half = plan.astype(jnp.bfloat16)
        live = lax.broadcasted_iota(jnp.int32, (tile_count, row_count), 1) < lengths_col
        for comp in range(3):
            load_ref[comp] = jnp.where(live, record_ref[5 + comp], 0.0)
        for comp in range(6):
            if comp == 0:
                rows = jnp.abs(record_ref[0])
            elif comp < 5:
                rows = record_ref[comp]
            else:
                rows = jnp.where(live, cell_ref[...], -1).astype(jnp.float32)
            high, rest = split_high(rows)
            middle, low = split_high(rest)
            total = None
            for part in (high, middle, low):
                term = jnp.dot(
                    plan_half, part.astype(jnp.bfloat16), preferred_element_type=jnp.float32
                )
                total = term if total is None else total + term
            out_ref[:, comp * row_count:(comp + 1) * row_count] = total

    def pack(routes, lengths, cell_ids, records):
        return pl.pallas_call(
            pack_kernel,
            out_shape=(
                jax.ShapeDtypeStruct((slot_total, 6 * row_count), jnp.float32),
                jax.ShapeDtypeStruct((3, tile_count, row_count), jnp.float32),
                jax.ShapeDtypeStruct((tile_count, slot_total), jnp.float32),
            ),
        )(routes.reshape(1, tile_count), lengths.reshape(1, tile_count), cell_ids, records)
    return pack


def unpack_kernel(plan_ref, returned_ref, load_ref, out_ref):
    plan = plan_ref[...].astype(jnp.bfloat16)
    high, rest = split_high(returned_ref[...])
    middle, low = split_high(rest)
    pressure = None
    for part in (high, middle, low):
        term = jnp.dot(plan, part.astype(jnp.bfloat16), preferred_element_type=jnp.float32)
        pressure = term if pressure is None else pressure + term
    for comp in range(out_ref.shape[0]):
        out_ref[comp] = load_ref[comp] * pressure


def shards(density, momentum_energy, viscosity, records, cell_ids, routes, lengths):
    fluid_state = jnp.concatenate([density[None], momentum_energy], 0)
    cells_x, cells_y, vertical_cells = density.shape
    plane_count = cells_x * cells_y
    tile_count = records.shape[1]
    row_count = records.shape[2]
    blocks = lax.axis_size("stream") * lax.axis_size("cross")
    capacity = max(2, 2 * tile_count // blocks)
    slot_total = blocks * capacity
    faces = slot_total * row_count

    pack = make_pack(tile_count, row_count, blocks, capacity)
    outbound, load_rows, placement_plan = pack(routes, lengths, cell_ids, records)
    arrived = lax.all_to_all(outbound, ("stream", "cross"), split_axis=0, concat_axis=0, tiled=True)
    outbound, state_and_visc = lax.optimization_barrier(
        (outbound, jnp.concatenate([fluid_state, viscosity[None]], 0))
    )
    state_visc = face_halo(state_and_visc)
    state_pad = state_visc[0:5]
    visc_pad = state_visc[5]

    cells = jnp.round(arrived[:, 5 * row_count:]).astype(jnp.int32).reshape(faces)
    plane = cells // vertical_cells
    depth = cells % vertical_cells
    depth_hot = (
        depth[:, None] == lax.broadcasted_iota(jnp.int32, (faces, vertical_cells), 1)
    )
    plane_rows = plane[None, :] == lax.broadcasted_iota(jnp.int32, (plane_count, faces), 0)
    arrived_values = jnp.stack(
        [arrived[:, c * row_count:(c + 1) * row_count].reshape(faces) for c in range(5)], 0
    )
    spread = jnp.where(plane_rows[None], arrived_values[:, None, :], 0.0)
    source = jnp.einsum(
        "cpf,fd->cpd", spread, depth_hot.astype(jnp.float32), precision=lax.Precision.HIGH
    )
    source = source.reshape(5, cells_x, cells_y, vertical_cells)

    middle = shifted(state_pad, 1, 0, 0) + viscous(state_pad, visc_pad) + source
    middle_pad = face_halo(middle)
    new_state = middle + viscous(middle_pad, visc_pad)

    flat_state = new_state.reshape(5, plane_count, vertical_cells)
    kinetic = (
        flat_state[1] * flat_state[1]
        + flat_state[2] * flat_state[2]
        + flat_state[3] * flat_state[3]
    )
    pressure = 0.4 * (flat_state[4] - 0.5 * kinetic / flat_state[0])
    picked = exact_dot("fd,dp->fp", pressure.T, depth_hot.astype(jnp.bfloat16), False)
    plane_cols = plane[:, None] == lax.broadcasted_iota(jnp.int32, (faces, plane_count), 1)
    face_pressure = jnp.sum(jnp.where(plane_cols, picked, 0.0), axis=1)
    returned = lax.all_to_all(
        face_pressure.reshape(1, slot_total, row_count),
        ("stream", "cross"),
        split_axis=1,
        concat_axis=1,
        tiled=True,
    )
    face_loads = pl.pallas_call(
        unpack_kernel, out_shape=jax.ShapeDtypeStruct(load_rows.shape, jnp.float32)
    )(placement_plan, returned[0], load_rows)
    return (new_state, face_loads)


def solution(mesh):
    placed = (
        P("stream", "cross", "gore"),
        P(None, "stream", "cross", "gore"),
        P("stream", "cross", "gore"),
        P(None, ("stream", "cross", "gore"), None),
        P(("stream", "cross", "gore"), None),
        P(("stream", "cross", "gore"), None),
        P(("stream", "cross", "gore")),
    )
    return jax.shard_map(
        shards,
        mesh=mesh,
        in_specs=placed,
        out_specs=(P(None, "stream", "cross", "gore"), P(None, ("stream", "cross", "gore"), None)),
        check_vma=False,
    )
```

```python
import jax
import jax.numpy as jnp
from jax import lax
from jax.experimental import pallas as pl
from jax.sharding import PartitionSpec as P


SIDES = (("stream", 1), ("cross", 2), ("gore", 3))


def face_halo(block):
    wide = block
    for axis, dim in SIDES:
        count = lax.axis_size(axis)
        index = lax.axis_index(axis)
        odd = index % 2 == 1
        extent = block.shape[dim]
        last = lax.slice_in_dim(block, extent - 1, None, axis=dim)
        first = lax.slice_in_dim(block, 0, 1, axis=dim)
        pairs_a = [(i, i ^ 1) for i in range(count) if (i ^ 1) < count]
        pairs_b = [(i, j) for i in range(1, count) for j in (i - 1, i + 1) if j >= 1 and j < count and (min(i, j) % 2 == 1)]
        from_a = lax.ppermute(jnp.where(odd, first, last), axis, pairs_a)
        if pairs_b:
            from_b = lax.ppermute(jnp.where(odd, last, first), axis, pairs_b)
        else:
            from_b = jnp.zeros_like(from_a)
        low = jnp.where(odd, from_a, from_b)
        high = jnp.where(odd, from_b, from_a)
        widths = [(0, 0)] + [(1, 1) if d < dim else (0, 0) for d in range(1, 4)]
        wide = jnp.concatenate([jnp.pad(low, widths), wide, jnp.pad(high, widths)], axis=dim)
    return wide


def harmonic(first_visc, second_visc):
    summed = first_visc + second_visc
    denominator = jnp.where(summed > 0, summed, 1.0)
    return 2.0 * first_visc * second_visc / denominator


def shifted(values, leading, spatial, offset):
    value_portions = [slice(None)] * leading
    for position in range(3):
        extent = values.shape[leading + position]
        if position == spatial:
            value_portions.append(slice(1 + offset, extent - 1 + offset))
        else:
            value_portions.append(slice(1, extent - 1))
    return values[tuple(value_portions)]


def viscous(field, visc):
    centre = shifted(field, 1, 0, 0)
    centre_visc = shifted(visc, 0, 0, 0)
    change = jnp.zeros_like(centre)
    for spatial in range(3):
        for offset in (1, -1):
            face_visc = harmonic(centre_visc, shifted(visc, 0, spatial, offset))
            change = change + face_visc[None] * (shifted(field, 1, spatial, offset) - centre)
    return change


def split_high(values):
    scaled = values * jnp.float32(65537.0)
    high = scaled - (scaled - values)
    return (high, values - high)


def three_bf16(values):
    first, rest = split_high(values)
    second, third = split_high(rest)
    return tuple(part.astype(jnp.bfloat16) for part in (first, second, third))


def exact_dot(spec, values, onehot, values_first):
    stacked = jnp.stack(three_bf16(values), 0)
    left, right = spec.split("->")[0].split(",")
    output = spec.split("->")[1]
    if values_first:
        terms = jnp.einsum(
            "k" + left + "," + right + "->k" + output, stacked, onehot,
            preferred_element_type=jnp.float32,
        )
    else:
        terms = jnp.einsum(
            left + ",k" + right + "->k" + output, onehot, stacked,
            preferred_element_type=jnp.float32,
        )
    return terms[0] + terms[1] + terms[2]


def make_pack(tile_count, row_count, blocks, capacity):
    slot_total = blocks * capacity

    def pack_kernel(route_ref, length_ref, cell_ref, record_ref, out_ref, load_ref, plan_ref):
        tile_iota_row = lax.broadcasted_iota(jnp.int32, (tile_count, tile_count), 1)
        tile_iota_col = lax.broadcasted_iota(jnp.int32, (tile_count, tile_count), 0)
        diagonal = tile_iota_row == tile_iota_col
        target = jnp.sum(jnp.where(diagonal, route_ref[...], 0), axis=1, keepdims=True)
        lengths_col = jnp.sum(jnp.where(diagonal, length_ref[...], 0), axis=1, keepdims=True)
        block_hot = (
            target == lax.broadcasted_iota(jnp.int32, (tile_count, blocks), 1)
        ).astype(jnp.float32)
        same = lax.dot_general(
            block_hot, block_hot, (((1,), (1,)), ((), ())), preferred_element_type=jnp.float32
        )
        rank = jnp.sum(jnp.where(tile_iota_row < tile_iota_col, same, 0.0), axis=1, keepdims=True)
        slot = target * capacity + rank.astype(jnp.int32)
        slot_hot = (
            slot == lax.broadcasted_iota(jnp.int32, (tile_count, slot_total), 1)
        ).astype(jnp.float32)
        plan_ref[...] = slot_hot
        eye = (
            lax.broadcasted_iota(jnp.int32, (slot_total, slot_total), 0)
            == lax.broadcasted_iota(jnp.int32, (slot_total, slot_total), 1)
        ).astype(jnp.float32)
        plan = lax.dot_general(
            eye, slot_hot, (((1,), (1,)), ((), ())), preferred_element_type=jnp.float32
        )
        plan_half = plan.astype(jnp.bfloat16)
        live = lax.broadcasted_iota(jnp.int32, (tile_count, row_count), 1) < lengths_col
        for comp in range(3):
            load_ref[comp] = jnp.where(live, record_ref[5 + comp], 0.0)
        for comp in range(6):
            if comp == 0:
                rows = jnp.abs(record_ref[0])
            elif comp < 5:
                rows = record_ref[comp]
            else:
                rows = jnp.where(live, cell_ref[...], -1).astype(jnp.float32)
            high, rest = split_high(rows)
            middle, low = split_high(rest)
            total = None
            for part in (high, middle, low):
                term = jnp.dot(
                    plan_half, part.astype(jnp.bfloat16), preferred_element_type=jnp.float32
                )
                total = term if total is None else total + term
            out_ref[:, comp * row_count:(comp + 1) * row_count] = total

    def pack(routes, lengths, cell_ids, records):
        return pl.pallas_call(
            pack_kernel,
            out_shape=(
                jax.ShapeDtypeStruct((slot_total, 6 * row_count), jnp.float32),
                jax.ShapeDtypeStruct((3, tile_count, row_count), jnp.float32),
                jax.ShapeDtypeStruct((tile_count, slot_total), jnp.float32),
            ),
        )(routes.reshape(1, tile_count), lengths.reshape(1, tile_count), cell_ids, records)
    return pack


def shards(density, momentum_energy, viscosity, records, cell_ids, routes, lengths):
    fluid_state = jnp.concatenate([density[None], momentum_energy], 0)
    cells_x, cells_y, vertical_cells = density.shape
    plane_count = cells_x * cells_y
    tile_count = records.shape[1]
    row_count = records.shape[2]
    blocks = lax.axis_size("stream") * lax.axis_size("cross")
    capacity = max(2, 2 * tile_count // blocks)
    slot_total = blocks * capacity
    faces = slot_total * row_count

    pack = make_pack(tile_count, row_count, blocks, capacity)
    outbound, load_rows, placement_plan = pack(routes, lengths, cell_ids, records)
    arrived = lax.all_to_all(outbound, ("stream", "cross"), split_axis=0, concat_axis=0, tiled=True)
    state_and_visc = jnp.concatenate([fluid_state, viscosity[None]], 0)
    state_visc = face_halo(state_and_visc)
    state_pad = state_visc[0:5]
    visc_pad = state_visc[5]

    cells = jnp.round(arrived[:, 5 * row_count:]).astype(jnp.int32).reshape(faces)
    plane = cells // vertical_cells
    depth = cells % vertical_cells
    depth_hot = (
        depth[:, None] == lax.broadcasted_iota(jnp.int32, (faces, vertical_cells), 1)
    )
    plane_rows = plane[None, :] == lax.broadcasted_iota(jnp.int32, (plane_count, faces), 0)
    arrived_values = jnp.stack(
        [arrived[:, c * row_count:(c + 1) * row_count].reshape(faces) for c in range(5)], 0
    )
    spread = jnp.where(plane_rows[None], arrived_values[:, None, :], 0.0)
    source = jnp.einsum(
        "cpf,fd->cpd", spread, depth_hot.astype(jnp.float32), precision=lax.Precision.HIGH
    )
    source = source.reshape(5, cells_x, cells_y, vertical_cells)

    middle = shifted(state_pad, 1, 0, 0) + viscous(state_pad, visc_pad) + source
    middle_pad = face_halo(middle)
    new_state = middle + viscous(middle_pad, visc_pad)

    flat_state = new_state.reshape(5, plane_count, vertical_cells)
    kinetic = (
        flat_state[1] * flat_state[1]
        + flat_state[2] * flat_state[2]
        + flat_state[3] * flat_state[3]
    )
    pressure = 0.4 * (flat_state[4] - 0.5 * kinetic / flat_state[0])
    picked = exact_dot("fd,dp->fp", pressure.T, depth_hot.astype(jnp.bfloat16), False)
    plane_cols = plane[:, None] == lax.broadcasted_iota(jnp.int32, (faces, plane_count), 1)
    face_pressure = jnp.sum(jnp.where(plane_cols, picked, 0.0), axis=1)
    returned = lax.all_to_all(
        face_pressure.reshape(1, slot_total, row_count),
        ("stream", "cross"),
        split_axis=1,
        concat_axis=1,
        tiled=True,
    )
    home_pressure = jnp.einsum(
        "ts,sr->tr", placement_plan, returned[0], precision=lax.Precision.HIGHEST
    )
    face_loads = load_rows * home_pressure[None]
    return (new_state, face_loads)


def solution(mesh):
    placed = (
        P("stream", "cross", "gore"),
        P(None, "stream", "cross", "gore"),
        P("stream", "cross", "gore"),
        P(None, ("stream", "cross", "gore"), None),
        P(("stream", "cross", "gore"), None),
        P(("stream", "cross", "gore"), None),
        P(("stream", "cross", "gore")),
    )
    return jax.shard_map(
        shards,
        mesh=mesh,
        in_specs=placed,
        out_specs=(P(None, "stream", "cross", "gore"), P(None, ("stream", "cross", "gore"), None)),
        check_vma=False,
    )
```
